256 devices in a mesh: dp: 4 (over x), node: 2 (over core), local: 32 (over z, y).
Axes of the slice: x: 4, y: 4, z: 8, core: 2. Of those that a mesh axis runs over, the one named last changes fastest.
Arguments:
- tokens: bfloat16 [32768, 2048], P(('dp', 'node', 'local')), may hold values from -6 to 6
- cotangent: bfloat16 [32768, 2048], P(('dp', 'node', 'local')), may hold values from -4 to 4
- routes: int32 [32768, 8], P(('dp', 'node', 'local')), may hold values from 0 to 63, all different within a row; in each aligned block of 128 rows (0 to 127, 128 to 255, ...) at most 24 rows name the same one
- gates: bfloat16 [32768, 8], P(('dp', 'node', 'local')), may hold values from 0.029907227 to 0.3984375
- w_gate: bfloat16 [64, 2048, 384], P(('node', 'local'), 'dp'), may hold values from -0.125 to 0.125
- w_up: bfloat16 [64, 2048, 384], P(('node', 'local'), 'dp'), may hold values from -0.125 to 0.125
- w_down: bfloat16 [64, 2048, 384], P(('node', 'local'), 'dp'), may hold values from -0.3125 to 0.3125
Outputs:
- input_grad: bfloat16 [32768, 2048], P(('dp', 'node', 'local'))
- gate_grad: bfloat16 [32768, 8], P(('dp', 'node', 'local'))
- gate_weight_grad: float32 [64, 2048, 384], P(('node', 'local'), 'dp')
- up_weight_grad: float32 [64, 2048, 384], P(('node', 'local'), 'dp')
- down_weight_grad: float32 [64, 2048, 384], P(('node', 'local'), 'dp')
The draws below stay inside these ranges and needn't reach their ends.
Inputs may be any that keep to these rules, and one draw needn't show every extreme that they name: `routes`: each token names 8 different experts. Among the tokens of one device no expert is named more than 24 times, and on some device some expert is named exactly 24 times.
All inputs are finite; a program needn't handle non-finite values.
Results may differ from the reference program's by a relative error of at most 0.0057.
Values may be sent and summed in bfloat16 or wider, within the bound.
No kernel may reach another device: no remote copies, remote signals or barrier semaphores. Data moves between devices by JAX's collectives and lax.ppermute only.
A program may use at most 128 MiB of HBM per device.

```python
import math
import jax
import jax.numpy as jnp
import numpy as np
from jax import lax

D = 2048
FF = 384
TOP = 8
TOK_DEV = 128
EXPERTS = 64
CAP = 24
TOKENS = 32768
N_DP = 4
N_NODE = 2
N_LOCAL = 32


def levels(rng, extent, cuts, low, top_value):
    gain, own = 1.0, jax.random.fold_in(rng, 6)
    for axis_at, shards_of in cuts:
        heights = jnp.exp(jax.random.uniform(jax.random.fold_in(own, axis_at), (shards_of,), jnp.float32, low / len(cuts), top_value / len(cuts)))
        gain = gain * jnp.repeat(heights, extent[axis_at] // shards_of).reshape([-1 if axis == axis_at else 1 for axis in range(len(extent))])
    return gain


def assign_block(key, own, number, rows, amount, top, limit, lean):
    sequence = jax.random.permutation(key, amount)
    crowded, usual = load_shares(amount, rows * top, limit, lean, True), load_shares(amount, rows * top, limit, lean, False)
    places = jnp.arange(amount)

    def named(tallies, turn):
        used = int((tallies > 0).sum())
        fixed = max(1, used // 4)
        shifted = fixed + (places - fixed + turn * (used - fixed)) % max(1, amount - fixed)
        return jnp.zeros((amount,), jnp.int32).at[sequence[jnp.where(places < fixed, places, shifted)]].set(jnp.asarray(tallies, jnp.int32))

    tallies = jnp.where(number % 4 == 0, named(crowded, number // 4), named(usual, number - number // 4 - 1))
    mixed = jax.random.permutation(jax.random.fold_in(own, 3), amount)
    donor, receiver = mixed[0:amount // 2 * 2:2], mixed[1:amount // 2 * 2:2]
    slack = jnp.minimum(tallies[donor] - 1, limit - tallies[receiver]) // 2
    slack = jnp.where((donor == sequence[0]) | (receiver == sequence[0]) | (tallies[receiver] == 0), 0, jnp.maximum(slack, 0))
    shifted = jax.random.randint(jax.random.fold_in(own, 4), (amount // 2,), 0, 1 << 20) % (slack + 1)
    tallies = tallies.at[donor].add(-shifted).at[receiver].add(shifted)
    members = jnp.searchsorted(jnp.cumsum(tallies), jnp.arange(rows * top), side="right").astype(jnp.int32)
    listing = members.reshape(top, rows).T
    listing = listing[jax.random.permutation(jax.random.fold_in(own, 1), rows)]
    turn = jax.random.randint(jax.random.fold_in(own, 2), (rows, 1), 0, top)
    return jnp.take_along_axis(listing, (jnp.arange(top)[None, :] + turn) % top, axis=1)


def load_shares(amount, total, bound, lean, full):
    weights = [(1 << 20) // math.isqrt(standing ** lean) + 1 for standing in range(1, amount + 1)]
    largest = bound if full else min(bound, max(-(-total // amount), total * weights[0] // sum(weights)))
    least = 1 if total - largest >= amount - 1 else 0
    holding, rest = [largest] + [least] * (amount - 1), total - largest - least * (amount - 1)
    while rest > 0:
        movable = [i for i in range(1, amount) if holding[i] < largest] or [i for i in range(1, amount) if holding[i] < bound]
        pool, budget = sum([weights[i] for i in movable]), rest
        for i in movable:
            extra = min(bound - holding[i], max(1, budget * weights[i] // pool), rest)
            holding[i] = holding[i] + extra
            rest = rest - extra
    return np.array(holding)


def centred(own_key, dims, scale, reach, pieces=(), kind=jnp.bfloat16):
    array = jax.random.normal(own_key, dims, jnp.float32) * scale
    if len(pieces) > 0:
        array = levels(own_key, dims, pieces, -0.22, 0.18) * array
    return jnp.clip(array, min=-reach, max=reach).astype(kind)


def setup_inputs(seed: int = 0) -> dict:
    streams_of = jax.random.split(jax.random.key(seed), 8)
    tokens = centred(streams_of[0], (TOKENS, D), 1.0, 6.0, ((0, 256),))
    cotangent = centred(streams_of[1], (TOKENS, D), 0.5, 4.0, ((0, 256),))
    routes_keys = jax.random.split(jax.random.fold_in(streams_of[2], 1), TOKENS // TOK_DEV)
    routes_turns = jax.random.permutation(jax.random.fold_in(streams_of[2], 3), TOKENS // TOK_DEV)
    routes = jax.vmap(lambda own, number: assign_block(jax.random.fold_in(streams_of[2], 2), own, number, TOK_DEV, EXPERTS, TOP, CAP, 2))(routes_keys, routes_turns).reshape((TOKENS, TOP))
    gates = jnp.clip(jnp.exp(math.log(0.3984375) - 2.5894505 * jax.random.uniform(streams_of[3], (TOKENS, TOP), jnp.float32) ** levels(streams_of[3], (TOKENS, TOP), ((0, 256),), -0.2, 0.2)), 0.029907227, 0.3984375).astype(jnp.bfloat16)
    w_gate = centred(streams_of[4], (EXPERTS, D, FF), D ** -0.5, 0.125, ((0, 64), (1, 4)))
    w_up = centred(streams_of[5], (EXPERTS, D, FF), D ** -0.5, 0.125, ((0, 64), (1, 4)))
    w_down = centred(streams_of[6], (EXPERTS, D, FF), FF ** -0.5, 0.3125, ((0, 64), (1, 4)))
    return dict(tokens=tokens, cotangent=cotangent, routes=routes, gates=gates, w_gate=w_gate, w_up=w_up, w_down=w_down)


def expert_rows(rows_x, rows_dy, rows_gate, gate_proj, up_proj, down_proj):
    pre_gate = jnp.dot(rows_x, gate_proj, preferred_element_type=jnp.float32)
    pre_up = jnp.dot(rows_x, up_proj, preferred_element_type=jnp.float32)
    gate_sigmoid = jax.nn.sigmoid(pre_gate)
    activated = pre_gate * gate_sigmoid
    hidden = activated * pre_up
    upstream = jnp.dot(rows_dy, down_proj, preferred_element_type=jnp.float32)
    gate_grad = jnp.sum(upstream * hidden, axis=1).astype(jnp.bfloat16)
    weight = rows_gate.astype(jnp.float32)[:, None]
    scaled_hidden = (weight * hidden).astype(jnp.bfloat16)
    hidden_grad = weight * upstream
    pre_gate_grad = (hidden_grad * pre_up * gate_sigmoid * (1.0 + pre_gate * (1.0 - gate_sigmoid))).astype(jnp.bfloat16)
    pre_up_grad = (hidden_grad * activated).astype(jnp.bfloat16)
    over_rows = (((0,), (0,)), ((), ()))
    down_grad = lax.dot_general(rows_dy, scaled_hidden, over_rows, preferred_element_type=jnp.float32)
    gate_wgrad = lax.dot_general(rows_x, pre_gate_grad, over_rows, preferred_element_type=jnp.float32)
    up_wgrad = lax.dot_general(rows_x, pre_up_grad, over_rows, preferred_element_type=jnp.float32)
    over_hidden = (((1,), (1,)), ((), ()))
    input_rows = lax.dot_general(pre_gate_grad, gate_proj, over_hidden, preferred_element_type=jnp.float32)
    input_rows = input_rows + lax.dot_general(pre_up_grad, up_proj, over_hidden, preferred_element_type=jnp.float32)
    return input_rows.astype(jnp.bfloat16), gate_grad, gate_wgrad, up_wgrad, down_grad


def reference(tokens, cotangent, routes, gates, w_gate, w_up, w_down):
    pick_count = TOKENS * TOP
    flat_routes = routes.reshape(pick_count)
    flat_gates = gates.reshape(pick_count)
    sorted_picks = jnp.argsort(flat_routes, stable=True).astype(jnp.int32)
    expert_ids = jnp.arange(EXPERTS, dtype=jnp.int32)
    counts = jnp.sum((flat_routes[:, None] == expert_ids[None, :]).astype(jnp.int32), axis=0)
    starts = (jnp.cumsum(counts) - counts).astype(jnp.int32)
    most_rows = CAP * N_DP * N_NODE * N_LOCAL
    picks_ext = jnp.concatenate([sorted_picks, jnp.zeros((most_rows,), jnp.int32)])

    def one_expert(running, expert):
        input_total, gate_total = running
        chosen = lax.dynamic_slice_in_dim(picks_ext, starts[expert], most_rows)
        is_valid = jnp.arange(most_rows, dtype=jnp.int32) < counts[expert]
        owner_token = chosen // TOP
        rows_x = jnp.where(is_valid[:, None], tokens[owner_token], jnp.zeros((), tokens.dtype))
        rows_dy = jnp.where(is_valid[:, None], cotangent[owner_token], jnp.zeros((), cotangent.dtype))
        rows_gate = jnp.where(is_valid, flat_gates[chosen], jnp.zeros((), gates.dtype))
        results = expert_rows(rows_x, rows_dy, rows_gate, w_gate[expert], w_up[expert], w_down[expert])
        input_total = input_total.at[owner_token].add(jnp.where(is_valid[:, None], results[0].astype(jnp.float32), jnp.float32(0.0)))
        gate_total = gate_total.at[chosen].add(jnp.where(is_valid, results[1].astype(jnp.float32), jnp.float32(0.0)))
        return (input_total, gate_total), (results[2], results[3], results[4])

    start_state = (jnp.zeros((TOKENS, D), jnp.float32), jnp.zeros((pick_count,), jnp.float32))
    final_state, weight_grads = lax.scan(one_expert, start_state, expert_ids)
    input_grad = final_state[0].astype(jnp.bfloat16)
    gate_grad = final_state[1].reshape(TOKENS, TOP).astype(jnp.bfloat16)
    return input_grad, gate_grad, weight_grads[0], weight_grads[1], weight_grads[2]
```

```python
import jax
import jax.numpy as jnp
from jax import lax
from jax.sharding import PartitionSpec as P


def expert_rows(rows_x, rows_dy, rows_gate, gate_proj, up_proj, down_proj):
    pre_gate = jnp.dot(rows_x, gate_proj, preferred_element_type=jnp.float32)
    pre_up = jnp.dot(rows_x, up_proj, preferred_element_type=jnp.float32)
    gate_sigmoid = jax.nn.sigmoid(pre_gate)
    activated = pre_gate * gate_sigmoid
    hidden = activated * pre_up
    upstream = jnp.dot(rows_dy, down_proj, preferred_element_type=jnp.float32)
    gate_grad = jnp.sum(upstream * hidden, axis=1).astype(jnp.bfloat16)
    weight = rows_gate.astype(jnp.float32)[:, None]
    scaled_hidden = (weight * hidden).astype(jnp.bfloat16)
    hidden_grad = weight * upstream
    pre_gate_grad = (
        hidden_grad * pre_up * gate_sigmoid * (1.0 + pre_gate * (1.0 - gate_sigmoid))
    ).astype(jnp.bfloat16)
    pre_up_grad = (hidden_grad * activated).astype(jnp.bfloat16)
    over_rows = (((0,), (0,)), ((), ()))
    down_grad = lax.dot_general(
        rows_dy, scaled_hidden, over_rows, preferred_element_type=jnp.float32
    )
    gate_wgrad = lax.dot_general(
        rows_x, pre_gate_grad, over_rows, preferred_element_type=jnp.float32
    )
    up_wgrad = lax.dot_general(rows_x, pre_up_grad, over_rows, preferred_element_type=jnp.float32)
    over_hidden = (((1,), (1,)), ((), ()))
    input_rows = lax.dot_general(
        pre_gate_grad, gate_proj, over_hidden, preferred_element_type=jnp.float32
    )
    input_rows = input_rows + lax.dot_general(
        pre_up_grad, up_proj, over_hidden, preferred_element_type=jnp.float32
    )
    return (input_rows.astype(jnp.bfloat16), gate_grad, gate_wgrad, up_wgrad, down_grad)


def local(tokens, cotangent, routes, gates, w_gate, w_up, w_down):
    tokens_dev, top_count = routes.shape
    width = tokens.shape[1]
    groups = lax.axis_size("node")
    members = lax.axis_size("local")
    experts = groups * members
    capacity = min(
        tokens_dev,
        max(3 * tokens_dev * top_count // (2 * experts), tokens_dev * top_count // experts),
    )
    slots = experts * capacity
    pad = 128
    hit = routes[:, :, None] == jnp.arange(experts, dtype=jnp.int32)[None, None, :]
    named = jnp.any(hit, axis=1)
    earlier = (
        jnp.arange(tokens_dev)[:, None] > jnp.arange(tokens_dev)[None, :]
    ).astype(jnp.bfloat16)
    rank = jnp.dot(earlier, named.astype(jnp.bfloat16), preferred_element_type=jnp.float32)
    rank = rank.astype(jnp.int32)
    choose = named.T[:, None, :] & (
        rank.T[:, None, :] == jnp.arange(capacity, dtype=jnp.int32)[None, :, None]
    )
    choose_b = choose.astype(jnp.bfloat16)
    send_x = jnp.einsum(
        "ert,td->erd", choose_b, tokens, preferred_element_type=jnp.float32
    ).astype(jnp.bfloat16)
    send_dy = jnp.einsum(
        "ert,td->erd", choose_b, cotangent, preferred_element_type=jnp.float32
    ).astype(jnp.bfloat16)
    gate_te = jnp.sum(jnp.where(hit, gates[:, :, None], jnp.zeros((), gates.dtype)), axis=1)
    send_gate = jnp.sum(
        jnp.where(choose, gate_te.T[:, None, :], jnp.zeros((), gates.dtype)), axis=2
    )
    gate_block = jnp.zeros((experts, capacity, pad), jnp.bfloat16).at[:, :, 0].set(send_gate)
    send = jnp.concatenate([send_x, send_dy, gate_block], axis=2)
    full_weights = (
        lax.all_gather(w_gate, "dp", axis=1, tiled=True),
        lax.all_gather(w_up, "dp", axis=1, tiled=True),
        lax.all_gather(w_down, "dp", axis=1, tiled=True),
    )
    gate_proj = full_weights[0][0]
    up_proj = full_weights[1][0]
    down_proj = full_weights[2][0]
    recv = lax.all_to_all(send, ("node", "local"), split_axis=0, concat_axis=0, tiled=True)
    flat = recv.reshape(slots, 2 * width + pad)
    results = expert_rows(
        flat[:, :width],
        flat[:, width : 2 * width],
        flat[:, 2 * width],
        gate_proj,
        up_proj,
        down_proj,
    )
    grad_block = jnp.zeros((slots, pad), jnp.bfloat16).at[:, 0].set(results[1])
    back = jnp.concatenate([results[0], grad_block], axis=1).reshape(
        experts, capacity, width + pad
    )
    home = lax.all_to_all(back, ("node", "local"), split_axis=0, concat_axis=0, tiled=True)
    input_grad = jnp.einsum(
        "ert,erd->td", choose_b, home[:, :, :width], preferred_element_type=jnp.float32
    ).astype(jnp.bfloat16)
    home_gate = home[:, :, width]
    gate_et = jnp.sum(
        jnp.where(choose, home_gate[:, :, None], jnp.zeros((), jnp.bfloat16)), axis=1
    )
    gate_grad = jnp.sum(
        jnp.where(hit, gate_et.T[:, None, :], jnp.zeros((), jnp.bfloat16)), axis=2
    )
    summed = (
        lax.psum_scatter(results[2], "dp", scatter_dimension=0, tiled=True),
        lax.psum_scatter(results[3], "dp", scatter_dimension=0, tiled=True),
        lax.psum_scatter(results[4], "dp", scatter_dimension=0, tiled=True),
    )
    return (input_grad, gate_grad, summed[0][None], summed[1][None], summed[2][None])


def solution(mesh):
    placed = (
        P(("dp", "node", "local"), None),
        P(("dp", "node", "local"), None),
        P(("dp", "node", "local"), None),
        P(("dp", "node", "local"), None),
        P(("node", "local"), "dp", None),
        P(("node", "local"), "dp", None),
        P(("node", "local"), "dp", None),
    )
    return jax.shard_map(
        local,
        mesh=mesh,
        in_specs=placed,
        out_specs=(
            P(("dp", "node", "local"), None),
            P(("dp", "node", "local"), None),
            P(("node", "local"), "dp", None),
            P(("node", "local"), "dp", None),
            P(("node", "local"), "dp", None),
        ),
        check_vma=False,
    )
```

```python
import jax
import jax.numpy as jnp
from jax import lax
from jax.sharding import PartitionSpec as P


def expert_rows(rows_x, rows_dy, rows_gate, gate_proj, up_proj, down_proj):
    pre_gate = jnp.dot(rows_x, gate_proj, preferred_element_type=jnp.float32)
    pre_up = jnp.dot(rows_x, up_proj, preferred_element_type=jnp.float32)
    gate_sigmoid = jax.nn.sigmoid(pre_gate)
    activated = pre_gate * gate_sigmoid
    hidden = activated * pre_up
    upstream = jnp.dot(rows_dy, down_proj, preferred_element_type=jnp.float32)
    gate_grad = jnp.sum(upstream * hidden, axis=1).astype(jnp.bfloat16)
    weight = rows_gate.astype(jnp.float32)[:, None]
    scaled_hidden = (weight * hidden).astype(jnp.bfloat16)
    hidden_grad = weight * upstream
    pre_gate_grad = (
        hidden_grad * pre_up * gate_sigmoid * (1.0 + pre_gate * (1.0 - gate_sigmoid))
    ).astype(jnp.bfloat16)
    pre_up_grad = (hidden_grad * activated).astype(jnp.bfloat16)
    over_rows = (((0,), (0,)), ((), ()))
    down_grad = lax.dot_general(
        rows_dy, scaled_hidden, over_rows, preferred_element_type=jnp.float32
    )
    gate_wgrad = lax.dot_general(
        rows_x, pre_gate_grad, over_rows, preferred_element_type=jnp.float32
    )
    up_wgrad = lax.dot_general(rows_x, pre_up_grad, over_rows, preferred_element_type=jnp.float32)
    over_hidden = (((1,), (1,)), ((), ()))
    input_rows = lax.dot_general(
        pre_gate_grad, gate_proj, over_hidden, preferred_element_type=jnp.float32
    )
    input_rows = input_rows + lax.dot_general(
        pre_up_grad, up_proj, over_hidden, preferred_element_type=jnp.float32
    )
    return (input_rows.astype(jnp.bfloat16), gate_grad, gate_wgrad, up_wgrad, down_grad)


def local(tokens, cotangent, routes, gates, w_gate, w_up, w_down):
    tokens_dev, top_count = routes.shape
    width = tokens.shape[1]
    hidden_units = w_gate.shape[2]
    cores = lax.axis_size("node")
    planes = lax.axis_size("lz")
    rows_of = lax.axis_size("ly")
    experts = cores * planes * rows_of
    capacity = min(
        tokens_dev,
        max(3 * tokens_dev * top_count // (2 * experts), tokens_dev * top_count // experts),
    )
    near = cores * rows_of
    slots = near * planes * capacity
    pad = 128
    meta = (
        jnp.zeros((tokens_dev, pad), jnp.bfloat16)
        .at[:, :top_count]
        .set(gates)
        .at[:, top_count : 2 * top_count]
        .set(routes.astype(jnp.bfloat16))
    )
    pack = jnp.concatenate([tokens, cotangent, meta], axis=1)
    gathered = lax.all_gather(pack, "lz", axis=0, tiled=False)
    seen_gates = gathered[:, :, 2 * width : 2 * width + top_count]
    seen_routes = gathered[:, :, 2 * width + top_count : 2 * width + 2 * top_count].astype(
        jnp.int32
    )
    plane = lax.axis_index("lz")
    near_ids = jnp.arange(near, dtype=jnp.int32)
    near_experts = (near_ids // rows_of) * (planes * rows_of) + plane * rows_of + near_ids % rows_of
    hit = seen_routes[..., None] == near_experts
    named = jnp.any(hit, axis=2)
    earlier = (
        jnp.arange(tokens_dev)[:, None] > jnp.arange(tokens_dev)[None, :]
    ).astype(jnp.bfloat16)
    rank = jnp.einsum(
        "ts,zsj->jzt", earlier, named.astype(jnp.bfloat16), preferred_element_type=jnp.float32
    ).astype(jnp.int32)
    choose = jnp.transpose(named, (2, 0, 1))[:, :, None, :] & (
        rank[:, :, None, :] == jnp.arange(capacity, dtype=jnp.int32)[None, None, :, None]
    )
    choose_b = choose.astype(jnp.bfloat16)
    send_rows = jnp.einsum(
        "jzrt,ztd->jzrd",
        choose_b,
        gathered[:, :, : 2 * width],
        preferred_element_type=jnp.float32,
    ).astype(jnp.bfloat16)
    gate_tj = jnp.sum(
        jnp.where(hit, seen_gates[..., None], jnp.zeros((), jnp.bfloat16)), axis=2
    )
    send_gate = jnp.sum(
        jnp.where(
            choose, jnp.transpose(gate_tj, (2, 0, 1))[:, :, None, :], jnp.zeros((), jnp.bfloat16)
        ),
        axis=3,
    )
    gate_block = (
        jnp.zeros((near, planes, capacity, pad), jnp.bfloat16).at[..., 0].set(send_gate)
    )
    send = jnp.concatenate([send_rows, gate_block], axis=3)
    all_weights = lax.all_gather(
        jnp.concatenate([w_gate, w_up, w_down], axis=2), "dp", axis=1, tiled=True
    )[0]
    gate_proj = all_weights[:, :hidden_units]
    up_proj = all_weights[:, hidden_units : 2 * hidden_units]
    down_proj = all_weights[:, 2 * hidden_units :]
    recv = lax.all_to_all(send, ("node", "ly"), split_axis=0, concat_axis=0, tiled=True)
    flat = recv.reshape(slots, 2 * width + pad)
    results = expert_rows(
        flat[:, :width],
        flat[:, width : 2 * width],
        flat[:, 2 * width],
        gate_proj,
        up_proj,
        down_proj,
    )
    grad_block = jnp.zeros((slots, pad), jnp.bfloat16).at[:, 0].set(results[1])
    back = jnp.concatenate([results[0], grad_block], axis=1).reshape(
        near, planes, capacity, width + pad
    )
    home = lax.all_to_all(back, ("node", "ly"), split_axis=0, concat_axis=0, tiled=True)
    partial = jnp.einsum(
        "jzrt,jzrd->ztd", choose_b, home[..., :width], preferred_element_type=jnp.float32
    )
    gate_jzt = jnp.sum(
        jnp.where(choose, home[..., width][..., None], jnp.zeros((), jnp.bfloat16)), axis=2
    )
    pick_gate = jnp.sum(
        jnp.where(
            hit, jnp.transpose(gate_jzt, (1, 2, 0))[:, :, None, :], jnp.zeros((), jnp.bfloat16)
        ),
        axis=3,
    )
    gate_cols = (
        jnp.zeros((planes, tokens_dev, pad), jnp.float32)
        .at[..., :top_count]
        .set(pick_gate.astype(jnp.float32))
    )
    reduced = lax.psum_scatter(
        jnp.concatenate([partial, gate_cols], axis=2), "lz", scatter_dimension=0, tiled=True
    )[0]
    input_grad = reduced[:, :width].astype(jnp.bfloat16)
    gate_grad = reduced[:, width : width + top_count].astype(jnp.bfloat16)
    summed = lax.psum_scatter(
        jnp.concatenate([results[2], results[3], results[4]], axis=1),
        "dp",
        scatter_dimension=0,
        tiled=True,
    )
    return (
        input_grad,
        gate_grad,
        summed[None, :, :hidden_units],
        summed[None, :, hidden_units : 2 * hidden_units],
        summed[None, :, 2 * hidden_units :],
    )


def solution(mesh):
    local_size = mesh.shape["local"]
    rows_of = 4 if local_size % 4 == 0 else 1
    split = jax.sharding.Mesh(
        mesh.devices.reshape(
            mesh.shape["dp"], mesh.shape["node"], local_size // rows_of, rows_of
        ),
        ("dp", "node", "lz", "ly"),
    )
    rows = P(("dp", "node", "lz", "ly"), None)
    expert = P(("node", "lz", "ly"), "dp", None)
    return jax.shard_map(
        local,
        mesh=split,
        in_specs=(rows, rows, rows, rows, expert, expert, expert),
        out_specs=(rows, rows, expert, expert, expert),
        check_vma=False,
    )
```

```python
import jax
import jax.numpy as jnp
from jax import lax
from jax.sharding import PartitionSpec as P


def expert_rows(rows_x, rows_dy, rows_gate, gate_proj, up_proj, down_proj):
    pre_gate = jnp.dot(rows_x, gate_proj, preferred_element_type=jnp.float32)
    pre_up = jnp.dot(rows_x, up_proj, preferred_element_type=jnp.float32)
    gate_sigmoid = jax.nn.sigmoid(pre_gate)
    activated = pre_gate * gate_sigmoid
    hidden = activated * pre_up
    upstream = jnp.dot(rows_dy, down_proj, preferred_element_type=jnp.float32)
    gate_grad = jnp.sum(upstream * hidden, axis=1).astype(jnp.bfloat16)
    weight = rows_gate.astype(jnp.float32)[:, None]
    scaled_hidden = (weight * hidden).astype(jnp.bfloat16)
    hidden_grad = weight * upstream
    pre_gate_grad = (
        hidden_grad * pre_up * gate_sigmoid * (1.0 + pre_gate * (1.0 - gate_sigmoid))
    ).astype(jnp.bfloat16)
    pre_up_grad = (hidden_grad * activated).astype(jnp.bfloat16)
    over_hidden = (((1,), (1,)), ((), ()))
    input_rows = lax.dot_general(
        pre_gate_grad, gate_proj, over_hidden, preferred_element_type=jnp.float32
    )
    input_rows = input_rows + lax.dot_general(
        pre_up_grad, up_proj, over_hidden, preferred_element_type=jnp.float32
    )
    return input_rows.astype(jnp.bfloat16), gate_grad, pre_gate_grad, pre_up_grad, scaled_hidden


def weight_grads(rows_x, rows_dy, pre_gate_grad, pre_up_grad, scaled_hidden):
    over_rows = (((0,), (0,)), ((), ()))
    down_grad = lax.dot_general(
        rows_dy, scaled_hidden, over_rows, preferred_element_type=jnp.float32
    )
    gate_wgrad = lax.dot_general(
        rows_x, pre_gate_grad, over_rows, preferred_element_type=jnp.float32
    )
    up_wgrad = lax.dot_general(rows_x, pre_up_grad, over_rows, preferred_element_type=jnp.float32)
    return gate_wgrad, up_wgrad, down_grad


def local(tokens, cotangent, routes, gates, w_gate, w_up, w_down):
    tokens_dev, top_count = routes.shape
    width = tokens.shape[1]
    hidden_units = w_gate.shape[2]
    cores = lax.axis_size("node")
    planes = lax.axis_size("lz")
    rows_of = lax.axis_size("ly")
    experts = cores * planes * rows_of
    capacity = min(
        tokens_dev,
        max(3 * tokens_dev * top_count // (2 * experts), tokens_dev * top_count // experts),
    )
    near = cores * rows_of
    pad = 128
    meta = (
        jnp.zeros((tokens_dev, pad), jnp.bfloat16)
        .at[:, :top_count]
        .set(gates)
        .at[:, top_count : 2 * top_count]
        .set(routes.astype(jnp.bfloat16))
    )
    pack = jnp.concatenate([tokens, cotangent, meta], axis=1)
    all_weights = lax.all_gather(
        jnp.concatenate([w_gate, w_up, w_down], axis=2), "dp", axis=1, tiled=True
    )[0]
    gate_proj = all_weights[:, :hidden_units]
    up_proj = all_weights[:, hidden_units : 2 * hidden_units]
    down_proj = all_weights[:, 2 * hidden_units :]
    plane = lax.axis_index("lz")
    near_ids = jnp.arange(near, dtype=jnp.int32)
    near_experts = (near_ids // rows_of) * (planes * rows_of) + plane * rows_of + near_ids % rows_of
    earlier = (
        jnp.arange(tokens_dev)[:, None] > jnp.arange(tokens_dev)[None, :]
    ).astype(jnp.bfloat16)
    to_right = [(i, (i + 1) % planes) for i in range(planes)]
    to_left = [(i, (i - 1) % planes) for i in range(planes)]
    rounds = [([0], [pack])]
    right, left = pack, pack
    for step in range(1, (planes - 1) // 2 + 1):
        right = lax.ppermute(right, "lz", to_right)
        left = lax.ppermute(left, "lz", to_left)
        rounds.append(([-step, step], [right, left]))
    if planes % 2 == 0 and planes > 1:
        right = lax.ppermute(right, "lz", to_right)
        rounds.append(([planes // 2], [right]))
    partial_of = {}
    kept = []
    for offsets, packs in rounds:
        count = len(offsets)
        seen = jnp.stack(packs)
        seen_gates = seen[:, :, 2 * width : 2 * width + top_count]
        seen_routes = seen[:, :, 2 * width + top_count : 2 * width + 2 * top_count].astype(
            jnp.int32
        )
        hit = seen_routes[..., None] == near_experts
        named = jnp.any(hit, axis=2)
        rank = jnp.einsum(
            "ts,zsj->jzt",
            earlier,
            named.astype(jnp.bfloat16),
            preferred_element_type=jnp.float32,
        ).astype(jnp.int32)
        choose = jnp.transpose(named, (2, 0, 1))[:, :, None, :] & (
            rank[:, :, None, :] == jnp.arange(capacity, dtype=jnp.int32)[None, None, :, None]
        )
        choose_b = choose.astype(jnp.bfloat16)
        send_rows = jnp.einsum(
            "jzrt,ztd->jzrd",
            choose_b,
            seen[:, :, : 2 * width],
            preferred_element_type=jnp.float32,
        ).astype(jnp.bfloat16)
        gate_tj = jnp.sum(
            jnp.where(hit, seen_gates[..., None], jnp.zeros((), jnp.bfloat16)), axis=2
        )
        send_gate = jnp.sum(
            jnp.where(
                choose,
                jnp.transpose(gate_tj, (2, 0, 1))[:, :, None, :],
                jnp.zeros((), jnp.bfloat16),
            ),
            axis=3,
        )
        gate_block = (
            jnp.zeros((near, count, capacity, pad), jnp.bfloat16).at[..., 0].set(send_gate)
        )
        send = jnp.concatenate([send_rows, gate_block], axis=3)
        recv = lax.all_to_all(send, ("node", "ly"), split_axis=0, concat_axis=0, tiled=True)
        flat = recv.reshape(near * count * capacity, 2 * width + pad)
        rows_x = flat[:, :width]
        rows_dy = flat[:, width : 2 * width]
        results = expert_rows(
            rows_x, rows_dy, flat[:, 2 * width], gate_proj, up_proj, down_proj
        )
        kept.append((rows_x, rows_dy) + results[2:])
        grad_block = (
            jnp.zeros((near * count * capacity, pad), jnp.bfloat16).at[:, 0].set(results[1])
        )
        back = jnp.concatenate([results[0], grad_block], axis=1).reshape(
            near, count, capacity, width + pad
        )
        home = lax.all_to_all(back, ("node", "ly"), split_axis=0, concat_axis=0, tiled=True)
        partial = jnp.einsum(
            "jzrt,jzrd->ztd", choose_b, home[..., :width], preferred_element_type=jnp.float32
        )
        gate_jzt = jnp.sum(
            jnp.where(choose, home[..., width][..., None], jnp.zeros((), jnp.bfloat16)),
            axis=2,
        )
        pick_gate = jnp.sum(
            jnp.where(
                hit,
                jnp.transpose(gate_jzt, (1, 2, 0))[:, :, None, :],
                jnp.zeros((), jnp.bfloat16),
            ),
            axis=3,
        )
        gate_cols = (
            jnp.zeros((count, tokens_dev, pad), jnp.float32)
            .at[..., :top_count]
            .set(pick_gate.astype(jnp.float32))
        )
        joined = jnp.concatenate([partial, gate_cols], axis=2)
        for index, offset in enumerate(offsets):
            partial_of[offset % planes] = joined[index]
    stacked = jnp.stack([partial_of[m] for m in range(planes)])
    ordered = jnp.roll(stacked, plane, axis=0)
    reduced = lax.psum_scatter(ordered, "lz", scatter_dimension=0, tiled=True)[0]
    input_grad = reduced[:, :width].astype(jnp.bfloat16)
    gate_grad = reduced[:, width : width + top_count].astype(jnp.bfloat16)
    all_rows = [jnp.concatenate(parts, axis=0) for parts in zip(*kept)]
    grads = weight_grads(*all_rows)
    summed = lax.psum_scatter(
        jnp.concatenate(grads, axis=1), "dp", scatter_dimension=0, tiled=True
    )
    return (
        input_grad,
        gate_grad,
        summed[None, :, :hidden_units],
        summed[None, :, hidden_units : 2 * hidden_units],
        summed[None, :, 2 * hidden_units :],
    )


def solution(mesh):
    local_size = mesh.shape["local"]
    rows_of = 4 if local_size % 4 == 0 else 1
    split = jax.sharding.Mesh(
        mesh.devices.reshape(
            mesh.shape["dp"], mesh.shape["node"], local_size // rows_of, rows_of
        ),
        ("dp", "node", "lz", "ly"),
    )
    rows = P(("dp", "node", "lz", "ly"), None)
    expert = P(("node", "lz", "ly"), "dp", None)
    return jax.shard_map(
        local,
        mesh=split,
        in_specs=(rows, rows, rows, rows, expert, expert, expert),
        out_specs=(rows, rows, expert, expert, expert),
        check_vma=False,
    )
```

```python
import jax
import jax.numpy as jnp
from jax import lax
from jax.sharding import PartitionSpec as P


def expert_rows(rows_x, rows_dy, rows_gate, gate_proj, up_proj, down_proj):
    pre_gate = jnp.dot(rows_x, gate_proj, preferred_element_type=jnp.float32)
    pre_up = jnp.dot(rows_x, up_proj, preferred_element_type=jnp.float32)
    gate_sigmoid = jax.nn.sigmoid(pre_gate)
    activated = pre_gate * gate_sigmoid
    hidden = activated * pre_up
    upstream = jnp.dot(rows_dy, down_proj, preferred_element_type=jnp.float32)
    gate_grad = jnp.sum(upstream * hidden, axis=1).astype(jnp.bfloat16)
    weight = rows_gate.astype(jnp.float32)[:, None]
    scaled_hidden = (weight * hidden).astype(jnp.bfloat16)
    hidden_grad = weight * upstream
    pre_gate_grad = (
        hidden_grad * pre_up * gate_sigmoid * (1.0 + pre_gate * (1.0 - gate_sigmoid))
    ).astype(jnp.bfloat16)
    pre_up_grad = (hidden_grad * activated).astype(jnp.bfloat16)
    over_rows = (((0,), (0,)), ((), ()))
    down_grad = lax.dot_general(
        rows_dy, scaled_hidden, over_rows, preferred_element_type=jnp.float32
    )
    gate_wgrad = lax.dot_general(
        rows_x, pre_gate_grad, over_rows, preferred_element_type=jnp.float32
    )
    up_wgrad = lax.dot_general(rows_x, pre_up_grad, over_rows, preferred_element_type=jnp.float32)
    over_hidden = (((1,), (1,)), ((), ()))
    input_rows = lax.dot_general(
        pre_gate_grad, gate_proj, over_hidden, preferred_element_type=jnp.float32
    )
    input_rows = input_rows + lax.dot_general(
        pre_up_grad, up_proj, over_hidden, preferred_element_type=jnp.float32
    )
    return (input_rows.astype(jnp.bfloat16), gate_grad, gate_wgrad, up_wgrad, down_grad)


def local(tokens, cotangent, routes, gates, w_gate, w_up, w_down):
    tokens_dev, top_count = routes.shape
    width = tokens.shape[1]
    hidden_units = w_gate.shape[2]
    cores = lax.axis_size("node")
    planes = lax.axis_size("lz")
    rows_of = lax.axis_size("ly")
    experts = cores * planes * rows_of
    capacity = min(
        tokens_dev,
        max(3 * tokens_dev * top_count // (2 * experts), tokens_dev * top_count // experts),
    )
    near = cores * rows_of
    slots = near * planes * capacity
    pad = 128
    half = width // 2
    meta = (
        jnp.zeros((tokens_dev, pad), jnp.bfloat16)
        .at[:, :top_count]
        .set(gates)
        .at[:, top_count : 2 * top_count]
        .set(routes.astype(jnp.bfloat16))
    )
    seen_x = lax.all_gather(jnp.concatenate([tokens, meta], axis=1), "lz", axis=0, tiled=False)
    seen_dy = lax.all_gather(cotangent, "lz", axis=0, tiled=False)
    seen_gates = seen_x[:, :, width : width + top_count]
    seen_routes = seen_x[:, :, width + top_count : width + 2 * top_count].astype(jnp.int32)
    plane = lax.axis_index("lz")
    near_ids = jnp.arange(near, dtype=jnp.int32)
    near_experts = (near_ids // rows_of) * (planes * rows_of) + plane * rows_of + near_ids % rows_of
    hit = seen_routes[..., None] == near_experts
    named = jnp.any(hit, axis=2)
    earlier = (
        jnp.arange(tokens_dev)[:, None] > jnp.arange(tokens_dev)[None, :]
    ).astype(jnp.bfloat16)
    rank = jnp.einsum(
        "ts,zsj->jzt", earlier, named.astype(jnp.bfloat16), preferred_element_type=jnp.float32
    ).astype(jnp.int32)
    choose = jnp.transpose(named, (2, 0, 1))[:, :, None, :] & (
        rank[:, :, None, :] == jnp.arange(capacity, dtype=jnp.int32)[None, None, :, None]
    )
    choose_b = choose.astype(jnp.bfloat16)
    gate_tj = jnp.sum(
        jnp.where(hit, seen_gates[..., None], jnp.zeros((), jnp.bfloat16)), axis=2
    )
    send_gate = jnp.sum(
        jnp.where(
            choose, jnp.transpose(gate_tj, (2, 0, 1))[:, :, None, :], jnp.zeros((), jnp.bfloat16)
        ),
        axis=3,
    )
    gate_block = (
        jnp.zeros((near, planes, capacity, pad), jnp.bfloat16).at[..., 0].set(send_gate)
    )
    send_x = jnp.einsum(
        "jzrt,ztd->jzrd", choose_b, seen_x[:, :, :width], preferred_element_type=jnp.float32
    ).astype(jnp.bfloat16)
    send_x = jnp.concatenate([send_x, gate_block], axis=3)
    send_dy = jnp.einsum(
        "jzrt,ztd->jzrd", choose_b, seen_dy, preferred_element_type=jnp.float32
    ).astype(jnp.bfloat16)
    all_weights = lax.all_gather(
        jnp.concatenate([w_gate, w_up, w_down], axis=2), "dp", axis=1, tiled=True
    )[0]
    gate_proj = all_weights[:, :hidden_units]
    up_proj = all_weights[:, hidden_units : 2 * hidden_units]
    down_proj = all_weights[:, 2 * hidden_units :]
    recv_x = lax.all_to_all(send_x, ("node", "ly"), split_axis=0, concat_axis=0, tiled=True)
    recv_dy = lax.all_to_all(send_dy, ("node", "ly"), split_axis=0, concat_axis=0, tiled=True)
    flat_x = recv_x.reshape(slots, width + pad)
    results = expert_rows(
        flat_x[:, :width],
        recv_dy.reshape(slots, width),
        flat_x[:, width],
        gate_proj,
        up_proj,
        down_proj,
    )
    grad_block = jnp.zeros((slots, pad), jnp.bfloat16).at[:, 0].set(results[1])
    back_lo = jnp.concatenate([results[0][:, :half], grad_block], axis=1).reshape(
        near, planes, capacity, half + pad
    )
    back_hi = results[0][:, half:].reshape(near, planes, capacity, width - half)
    home_lo = lax.all_to_all(back_lo, ("node", "ly"), split_axis=0, concat_axis=0, tiled=True)
    home_hi = lax.all_to_all(back_hi, ("node", "ly"), split_axis=0, concat_axis=0, tiled=True)
    partial_lo = jnp.einsum(
        "jzrt,jzrd->ztd", choose_b, home_lo[..., :half], preferred_element_type=jnp.float32
    )
    gate_jzt = jnp.sum(
        jnp.where(choose, home_lo[..., half][..., None], jnp.zeros((), jnp.bfloat16)), axis=2
    )
    pick_gate = jnp.sum(
        jnp.where(
            hit, jnp.transpose(gate_jzt, (1, 2, 0))[:, :, None, :], jnp.zeros((), jnp.bfloat16)
        ),
        axis=3,
    )
    gate_cols = (
        jnp.zeros((planes, tokens_dev, pad), jnp.float32)
        .at[..., :top_count]
        .set(pick_gate.astype(jnp.float32))
    )
    reduced_lo = lax.psum_scatter(
        jnp.concatenate([partial_lo, gate_cols], axis=2), "lz", scatter_dimension=0, tiled=True
    )[0]
    partial_hi = jnp.einsum(
        "jzrt,jzrd->ztd", choose_b, home_hi, preferred_element_type=jnp.float32
    )
    reduced_hi = lax.psum_scatter(partial_hi, "lz", scatter_dimension=0, tiled=True)[0]
    input_grad = jnp.concatenate(
        [reduced_lo[:, :half], reduced_hi], axis=1
    ).astype(jnp.bfloat16)
    gate_grad = reduced_lo[:, half : half + top_count].astype(jnp.bfloat16)
    summed = lax.psum_scatter(
        jnp.concatenate([results[2], results[3], results[4]], axis=1),
        "dp",
        scatter_dimension=0,
        tiled=True,
    )
    return (
        input_grad,
        gate_grad,
        summed[None, :, :hidden_units],
        summed[None, :, hidden_units : 2 * hidden_units],
        summed[None, :, 2 * hidden_units :],
    )


def solution(mesh):
    local_size = mesh.shape["local"]
    rows_of = 4 if local_size % 4 == 0 else 1
    split = jax.sharding.Mesh(
        mesh.devices.reshape(
            mesh.shape["dp"], mesh.shape["node"], local_size // rows_of, rows_of
        ),
        ("dp", "node", "lz", "ly"),
    )
    rows = P(("dp", "node", "lz", "ly"), None)
    expert = P(("node", "lz", "ly"), "dp", None)
    return jax.shard_map(
        local,
        mesh=split,
        in_specs=(rows, rows, rows, rows, expert, expert, expert),
        out_specs=(rows, rows, expert, expert, expert),
        check_vma=False,
    )
```

```python
import jax
import jax.numpy as jnp
from jax import lax
from jax.sharding import PartitionSpec as P


def expert_rows(rows_x, rows_dy, rows_gate, gate_proj, up_proj, down_proj):
    pre_gate = jnp.dot(rows_x, gate_proj, preferred_element_type=jnp.float32)
    pre_up = jnp.dot(rows_x, up_proj, preferred_element_type=jnp.float32)
    gate_sigmoid = jax.nn.sigmoid(pre_gate)
    activated = pre_gate * gate_sigmoid
    hidden = activated * pre_up
    upstream = jnp.dot(rows_dy, down_proj, preferred_element_type=jnp.float32)
    gate_grad = jnp.sum(upstream * hidden, axis=1).astype(jnp.bfloat16)
    weight = rows_gate.astype(jnp.float32)[:, None]
    scaled_hidden = (weight * hidden).astype(jnp.bfloat16)
    hidden_grad = weight * upstream
    pre_gate_grad = (
        hidden_grad * pre_up * gate_sigmoid * (1.0 + pre_gate * (1.0 - gate_sigmoid))
    ).astype(jnp.bfloat16)
    pre_up_grad = (hidden_grad * activated).astype(jnp.bfloat16)
    over_rows = (((0,), (0,)), ((), ()))
    down_grad = lax.dot_general(
        rows_dy, scaled_hidden, over_rows, preferred_element_type=jnp.float32
    )
    gate_wgrad = lax.dot_general(
        rows_x, pre_gate_grad, over_rows, preferred_element_type=jnp.float32
    )
    up_wgrad = lax.dot_general(rows_x, pre_up_grad, over_rows, preferred_element_type=jnp.float32)
    over_hidden = (((1,), (1,)), ((), ()))
    input_rows = lax.dot_general(
        pre_gate_grad, gate_proj, over_hidden, preferred_element_type=jnp.float32
    )
    input_rows = input_rows + lax.dot_general(
        pre_up_grad, up_proj, over_hidden, preferred_element_type=jnp.float32
    )
    return (input_rows.astype(jnp.bfloat16), gate_grad, gate_wgrad, up_wgrad, down_grad)


def local(tokens, cotangent, routes, gates, w_gate, w_up, w_down):
    tokens_dev, top_count = routes.shape
    width = tokens.shape[1]
    hidden_units = w_gate.shape[2]
    cores = lax.axis_size("node")
    planes = lax.axis_size("lz")
    rows_of = lax.axis_size("ly")
    experts = cores * planes * rows_of
    capacity = min(
        tokens_dev,
        max(3 * tokens_dev * top_count // (2 * experts), tokens_dev * top_count // experts),
    )
    near = cores * rows_of
    slots = near * planes * capacity
    pad = 128
    half = width // 2
    meta = (
        jnp.zeros((tokens_dev, pad), jnp.bfloat16)
        .at[:, :top_count]
        .set(gates)
        .at[:, top_count : 2 * top_count]
        .set(routes.astype(jnp.bfloat16))
    )
    seen_x = lax.all_gather(jnp.concatenate([tokens, meta], axis=1), "lz", axis=0, tiled=False)
    seen_dy = lax.all_gather(cotangent, "lz", axis=0, tiled=False)
    seen_gates = seen_x[:, :, width : width + top_count]
    seen_routes = seen_x[:, :, width + top_count : width + 2 * top_count].astype(jnp.int32)
    plane = lax.axis_index("lz")
    near_ids = jnp.arange(near, dtype=jnp.int32)
    near_experts = (near_ids // rows_of) * (planes * rows_of) + plane * rows_of + near_ids % rows_of
    hit = seen_routes[..., None] == near_experts
    named = jnp.any(hit, axis=2)
    earlier = (
        jnp.arange(tokens_dev)[:, None] > jnp.arange(tokens_dev)[None, :]
    ).astype(jnp.bfloat16)
    rank = jnp.einsum(
        "ts,zsj->jzt", earlier, named.astype(jnp.bfloat16), preferred_element_type=jnp.float32
    ).astype(jnp.int32)
    choose = jnp.transpose(named, (2, 0, 1))[:, :, None, :] & (
        rank[:, :, None, :] == jnp.arange(capacity, dtype=jnp.int32)[None, None, :, None]
    )
    choose_b = choose.astype(jnp.bfloat16)
    gate_tj = jnp.sum(
        jnp.where(hit, seen_gates[..., None], jnp.zeros((), jnp.bfloat16)), axis=2
    )
    send_gate = jnp.sum(
        jnp.where(
            choose, jnp.transpose(gate_tj, (2, 0, 1))[:, :, None, :], jnp.zeros((), jnp.bfloat16)
        ),
        axis=3,
    )
    gate_block = (
        jnp.zeros((near, planes, capacity, pad), jnp.bfloat16).at[..., 0].set(send_gate)
    )
    send_x = jnp.einsum(
        "jzrt,ztd->jzrd", choose_b, seen_x[:, :, :width], preferred_element_type=jnp.float32
    ).astype(jnp.bfloat16)
    send_x = jnp.concatenate([send_x, gate_block], axis=3)
    send_dy = jnp.einsum(
        "jzrt,ztd->jzrd", choose_b, seen_dy, preferred_element_type=jnp.float32
    ).astype(jnp.bfloat16)
    all_weights = lax.all_gather(
        jnp.concatenate([w_gate, w_up, w_down], axis=2), "dp", axis=1, tiled=True
    )[0]
    gate_proj = all_weights[:, :hidden_units]
    up_proj = all_weights[:, hidden_units : 2 * hidden_units]
    down_proj = all_weights[:, 2 * hidden_units :]
    recv_x = lax.all_to_all(send_x, ("node", "ly"), split_axis=0, concat_axis=0, tiled=True)
    recv_dy = lax.all_to_all(send_dy, ("node", "ly"), split_axis=0, concat_axis=0, tiled=True)
    flat_x = recv_x.reshape(slots, width + pad)
    results = expert_rows(
        flat_x[:, :width],
        recv_dy.reshape(slots, width),
        flat_x[:, width],
        gate_proj,
        up_proj,
        down_proj,
    )
    grad_block = jnp.zeros((slots, pad), jnp.bfloat16).at[:, 0].set(results[1])
    back_lo = jnp.concatenate([results[0][:, :half], grad_block], axis=1).reshape(
        near, planes, capacity, half + pad
    )
    back_hi = results[0][:, half:].reshape(near, planes, capacity, width - half)
    home_lo = lax.all_to_all(back_lo, ("node", "ly"), split_axis=0, concat_axis=0, tiled=True)
    home_hi = lax.all_to_all(back_hi, ("node", "ly"), split_axis=0, concat_axis=0, tiled=True)
    partial_lo = jnp.einsum(
        "jzrt,jzrd->ztd", choose_b, home_lo[..., :half], preferred_element_type=jnp.float32
    )
    gate_jzt = jnp.sum(
        jnp.where(choose, home_lo[..., half][..., None], jnp.zeros((), jnp.bfloat16)), axis=2
    )
    pick_gate = jnp.sum(
        jnp.where(
            hit, jnp.transpose(gate_jzt, (1, 2, 0))[:, :, None, :], jnp.zeros((), jnp.bfloat16)
        ),
        axis=3,
    )
    gate_cols = (
        jnp.zeros((planes, tokens_dev, pad), jnp.float32)
        .at[..., :top_count]
        .set(pick_gate.astype(jnp.float32))
    )
    summed = lax.psum_scatter(
        jnp.concatenate([results[2], results[3], results[4]], axis=1),
        "dp",
        scatter_dimension=0,
        tiled=True,
    )
    summed, partial_lo, gate_cols = lax.optimization_barrier((summed, partial_lo, gate_cols))
    reduced_lo = lax.psum_scatter(
        jnp.concatenate([partial_lo, gate_cols], axis=2), "lz", scatter_dimension=0, tiled=True
    )[0]
    partial_hi = jnp.einsum(
        "jzrt,jzrd->ztd", choose_b, home_hi, preferred_element_type=jnp.float32
    )
    reduced_hi = lax.psum_scatter(partial_hi, "lz", scatter_dimension=0, tiled=True)[0]
    input_grad = jnp.concatenate(
        [reduced_lo[:, :half], reduced_hi], axis=1
    ).astype(jnp.bfloat16)
    gate_grad = reduced_lo[:, half : half + top_count].astype(jnp.bfloat16)
    return (
        input_grad,
        gate_grad,
        summed[None, :, :hidden_units],
        summed[None, :, hidden_units : 2 * hidden_units],
        summed[None, :, 2 * hidden_units :],
    )


def solution(mesh):
    local_size = mesh.shape["local"]
    rows_of = 4 if local_size % 4 == 0 else 1
    split = jax.sharding.Mesh(
        mesh.devices.reshape(
            mesh.shape["dp"], mesh.shape["node"], local_size // rows_of, rows_of
        ),
        ("dp", "node", "lz", "ly"),
    )
    rows = P(("dp", "node", "lz", "ly"), None)
    expert = P(("node", "lz", "ly"), "dp", None)
    return jax.shard_map(
        local,
        mesh=split,
        in_specs=(rows, rows, rows, rows, expert, expert, expert),
        out_specs=(rows, rows, expert, expert, expert),
        check_vma=False,
    )
```

```python
import jax
import jax.numpy as jnp
from jax import lax
from jax.sharding import PartitionSpec as P


def expert_rows(rows_x, rows_dy, rows_gate, gate_proj, up_proj, down_proj):
    pre_gate = jnp.dot(rows_x, gate_proj, preferred_element_type=jnp.float32)
    pre_up = jnp.dot(rows_x, up_proj, preferred_element_type=jnp.float32)
    gate_sigmoid = jax.nn.sigmoid(pre_gate)
    activated = pre_gate * gate_sigmoid
    hidden = activated * pre_up
    upstream = jnp.dot(rows_dy, down_proj, preferred_element_type=jnp.float32)
    gate_grad = jnp.sum(upstream * hidden, axis=1).astype(jnp.bfloat16)
    weight = rows_gate.astype(jnp.float32)[:, None]
    scaled_hidden = (weight * hidden).astype(jnp.bfloat16)
    hidden_grad = weight * upstream
    pre_gate_grad = (
        hidden_grad * pre_up * gate_sigmoid * (1.0 + pre_gate * (1.0 - gate_sigmoid))
    ).astype(jnp.bfloat16)
    pre_up_grad = (hidden_grad * activated).astype(jnp.bfloat16)
    over_rows = (((0,), (0,)), ((), ()))
    down_grad = lax.dot_general(
        rows_dy, scaled_hidden, over_rows, preferred_element_type=jnp.float32
    )
    gate_wgrad = lax.dot_general(
        rows_x, pre_gate_grad, over_rows, preferred_element_type=jnp.float32
    )
    up_wgrad = lax.dot_general(rows_x, pre_up_grad, over_rows, preferred_element_type=jnp.float32)
    over_hidden = (((1,), (1,)), ((), ()))
    input_rows = lax.dot_general(
        pre_gate_grad, gate_proj, over_hidden, preferred_element_type=jnp.float32
    )
    input_rows = input_rows + lax.dot_general(
        pre_up_grad, up_proj, over_hidden, preferred_element_type=jnp.float32
    )
    return (input_rows.astype(jnp.bfloat16), gate_grad, gate_wgrad, up_wgrad, down_grad)


def local(tokens, cotangent, routes, gates, w_gate, w_up, w_down):
    tokens_dev, top_count = routes.shape
    width = tokens.shape[1]
    hidden_units = w_gate.shape[2]
    cores = lax.axis_size("node")
    planes = lax.axis_size("lz")
    rows_of = lax.axis_size("ly")
    experts = cores * planes * rows_of
    capacity = min(
        tokens_dev,
        max(3 * tokens_dev * top_count // (2 * experts), tokens_dev * top_count // experts),
    )
    near = cores * rows_of
    slots = near * planes * capacity
    pad = 128
    half = width // 2
    meta = (
        jnp.zeros((tokens_dev, pad), jnp.bfloat16)
        .at[:, :top_count]
        .set(gates)
        .at[:, top_count : 2 * top_count]
        .set(routes.astype(jnp.bfloat16))
    )
    seen_x = lax.all_gather(jnp.concatenate([tokens, meta], axis=1), "lz", axis=0, tiled=False)
    seen_dy = lax.all_gather(cotangent, "lz", axis=0, tiled=False)
    seen_gates = seen_x[:, :, width : width + top_count]
    seen_routes = seen_x[:, :, width + top_count : width + 2 * top_count].astype(jnp.int32)
    plane = lax.axis_index("lz")
    near_ids = jnp.arange(near, dtype=jnp.int32)
    near_experts = (near_ids // rows_of) * (planes * rows_of) + plane * rows_of + near_ids % rows_of
    hit = seen_routes[..., None] == near_experts
    named = jnp.any(hit, axis=2)
    earlier = (
        jnp.arange(tokens_dev)[:, None] > jnp.arange(tokens_dev)[None, :]
    ).astype(jnp.bfloat16)
    rank = jnp.einsum(
        "ts,zsj->jzt", earlier, named.astype(jnp.bfloat16), preferred_element_type=jnp.float32
    ).astype(jnp.int32)
    choose = jnp.transpose(named, (2, 0, 1))[:, :, None, :] & (
        rank[:, :, None, :] == jnp.arange(capacity, dtype=jnp.int32)[None, None, :, None]
    )
    choose_b = choose.astype(jnp.bfloat16)
    gate_tj = jnp.sum(
        jnp.where(hit, seen_gates[..., None], jnp.zeros((), jnp.bfloat16)), axis=2
    )
    send_gate = jnp.sum(
        jnp.where(
            choose, jnp.transpose(gate_tj, (2, 0, 1))[:, :, None, :], jnp.zeros((), jnp.bfloat16)
        ),
        axis=3,
    )
    gate_block = (
        jnp.zeros((near, planes, capacity, pad), jnp.bfloat16).at[..., 0].set(send_gate)
    )
    send_x = jnp.einsum(
        "jzrt,ztd->jzrd", choose_b, seen_x[:, :, :width], preferred_element_type=jnp.float32
    ).astype(jnp.bfloat16)
    send_x = jnp.concatenate([send_x, gate_block], axis=3).reshape(
        near, planes * capacity, width + pad
    )
    send_dy = (
        jnp.einsum("jzrt,ztd->jzrd", choose_b, seen_dy, preferred_element_type=jnp.float32)
        .astype(jnp.bfloat16)
        .reshape(near, planes * capacity, width)
    )
    all_weights = lax.all_gather(
        jnp.concatenate([w_gate, w_up, w_down], axis=2), "dp", axis=1, tiled=True
    )[0]
    gate_proj = all_weights[:, :hidden_units]
    up_proj = all_weights[:, hidden_units : 2 * hidden_units]
    down_proj = all_weights[:, 2 * hidden_units :]
    recv_x = lax.all_to_all(send_x, ("node", "ly"), split_axis=0, concat_axis=0, tiled=True)
    recv_dy = lax.all_to_all(send_dy, ("node", "ly"), split_axis=0, concat_axis=0, tiled=True)
    flat_x = recv_x.reshape(slots, width + pad)
    results = expert_rows(
        flat_x[:, :width],
        recv_dy.reshape(slots, width),
        flat_x[:, width],
        gate_proj,
        up_proj,
        down_proj,
    )
    grad_block = jnp.zeros((slots, pad), jnp.bfloat16).at[:, 0].set(results[1])
    back_lo = jnp.concatenate([results[0][:, :half], grad_block], axis=1).reshape(
        near, planes * capacity, half + pad
    )
    back_hi = results[0][:, half:].reshape(near, planes * capacity, width - half)
    home_lo = lax.all_to_all(
        back_lo, ("node", "ly"), split_axis=0, concat_axis=0, tiled=True
    ).reshape(near, planes, capacity, half + pad)
    home_hi = lax.all_to_all(
        back_hi, ("node", "ly"), split_axis=0, concat_axis=0, tiled=True
    ).reshape(near, planes, capacity, width - half)
    partial_lo = jnp.einsum(
        "jzrt,jzrd->ztd", choose_b, home_lo[..., :half], preferred_element_type=jnp.float32
    )
    gate_jzt = jnp.sum(
        jnp.where(choose, home_lo[..., half][..., None], jnp.zeros((), jnp.bfloat16)), axis=2
    )
    pick_gate = jnp.sum(
        jnp.where(
            hit, jnp.transpose(gate_jzt, (1, 2, 0))[:, :, None, :], jnp.zeros((), jnp.bfloat16)
        ),
        axis=3,
    )
    gate_cols = (
        jnp.zeros((planes, tokens_dev, pad), jnp.float32)
        .at[..., :top_count]
        .set(pick_gate.astype(jnp.float32))
    )
    summed = lax.psum_scatter(
        jnp.concatenate([results[2], results[3], results[4]], axis=1),
        "dp",
        scatter_dimension=0,
        tiled=True,
    )
    summed, partial_lo, gate_cols = lax.optimization_barrier((summed, partial_lo, gate_cols))
    reduced_lo = lax.psum_scatter(
        jnp.concatenate([partial_lo, gate_cols], axis=2), "lz", scatter_dimension=0, tiled=True
    )[0]
    partial_hi = jnp.einsum(
        "jzrt,jzrd->ztd", choose_b, home_hi, preferred_element_type=jnp.float32
    )
    reduced_hi = lax.psum_scatter(partial_hi, "lz", scatter_dimension=0, tiled=True)[0]
    input_grad = jnp.concatenate(
        [reduced_lo[:, :half], reduced_hi], axis=1
    ).astype(jnp.bfloat16)
    gate_grad = reduced_lo[:, half : half + top_count].astype(jnp.bfloat16)
    return (
        input_grad,
        gate_grad,
        summed[None, :, :hidden_units],
        summed[None, :, hidden_units : 2 * hidden_units],
        summed[None, :, 2 * hidden_units :],
    )


def solution(mesh):
    local_size = mesh.shape["local"]
    rows_of = 4 if local_size % 4 == 0 else 1
    split = jax.sharding.Mesh(
        mesh.devices.reshape(
            mesh.shape["dp"], mesh.shape["node"], local_size // rows_of, rows_of
        ),
        ("dp", "node", "lz", "ly"),
    )
    rows = P(("dp", "node", "lz", "ly"), None)
    expert = P(("node", "lz", "ly"), "dp", None)
    return jax.shard_map(
        local,
        mesh=split,
        in_specs=(rows, rows, rows, rows, expert, expert, expert),
        out_specs=(rows, rows, expert, expert, expert),
        check_vma=False,
    )
```

```python
import jax
import jax.numpy as jnp
from jax import lax
from jax.sharding import PartitionSpec as P


def expert_rows(rows_x, rows_dy, rows_gate, gate_proj, up_proj, down_proj):
    pre_gate = jnp.dot(rows_x, gate_proj, preferred_element_type=jnp.float32)
    pre_up = jnp.dot(rows_x, up_proj, preferred_element_type=jnp.float32)
    gate_sigmoid = jax.nn.sigmoid(pre_gate)
    activated = pre_gate * gate_sigmoid
    hidden = activated * pre_up
    upstream = jnp.dot(rows_dy, down_proj, preferred_element_type=jnp.float32)
    gate_grad = jnp.sum(upstream * hidden, axis=1).astype(jnp.bfloat16)
    weight = rows_gate.astype(jnp.float32)[:, None]
    scaled_hidden = (weight * hidden).astype(jnp.bfloat16)
    hidden_grad = weight * upstream
    pre_gate_grad = (
        hidden_grad * pre_up * gate_sigmoid * (1.0 + pre_gate * (1.0 - gate_sigmoid))
    ).astype(jnp.bfloat16)
    pre_up_grad = (hidden_grad * activated).astype(jnp.bfloat16)
    over_rows = (((0,), (0,)), ((), ()))
    down_grad = lax.dot_general(
        rows_dy, scaled_hidden, over_rows, preferred_element_type=jnp.float32
    )
    gate_wgrad = lax.dot_general(
        rows_x, pre_gate_grad, over_rows, preferred_element_type=jnp.float32
    )
    up_wgrad = lax.dot_general(rows_x, pre_up_grad, over_rows, preferred_element_type=jnp.float32)
    over_hidden = (((1,), (1,)), ((), ()))
    input_rows = lax.dot_general(
        pre_gate_grad, gate_proj, over_hidden, preferred_element_type=jnp.float32
    )
    input_rows = input_rows + lax.dot_general(
        pre_up_grad, up_proj, over_hidden, preferred_element_type=jnp.float32
    )
    return (input_rows.astype(jnp.bfloat16), gate_grad, gate_wgrad, up_wgrad, down_grad)


def ring_sum_scatter(full):
    ring = lax.axis_size("dp")
    rank = lax.axis_index("dp")
    rows = full.shape[0] // ring
    split = full.shape[1] // 2
    to_right = [(i, (i + 1) % ring) for i in range(ring)]
    to_left = [(i, (i - 1) % ring) for i in range(ring)]

    def block(index, lo, hi):
        start = ((index % ring + ring) % ring) * rows
        return lax.dynamic_slice(full, (start, lo), (rows, hi - lo))

    width = full.shape[1]
    right = block(rank - 1, 0, split)
    left = block(rank + 1, split, width)
    for step in range(2, ring + 1):
        right = lax.ppermute(right, "dp", to_right) + block(rank - step, 0, split)
        left = lax.ppermute(left, "dp", to_left) + block(rank + step, split, width)
    return jnp.concatenate([right, left], axis=1)


def local(tokens, cotangent, routes, gates, w_gate, w_up, w_down):
    tokens_dev, top_count = routes.shape
    width = tokens.shape[1]
    hidden_units = w_gate.shape[2]
    cores = lax.axis_size("node")
    planes = lax.axis_size("lz")
    rows_of = lax.axis_size("ly")
    experts = cores * planes * rows_of
    capacity = min(
        tokens_dev,
        max(3 * tokens_dev * top_count // (2 * experts), tokens_dev * top_count // experts),
    )
    near = cores * rows_of
    slots = near * planes * capacity
    pad = 128
    half = width // 2
    meta = (
        jnp.zeros((tokens_dev, pad), jnp.bfloat16)
        .at[:, :top_count]
        .set(gates)
        .at[:, top_count : 2 * top_count]
        .set(routes.astype(jnp.bfloat16))
    )
    seen_x = lax.all_gather(jnp.concatenate([tokens, meta], axis=1), "lz", axis=0, tiled=False)
    seen_dy = lax.all_gather(cotangent, "lz", axis=0, tiled=False)
    seen_gates = seen_x[:, :, width : width + top_count]
    seen_routes = seen_x[:, :, width + top_count : width + 2 * top_count].astype(jnp.int32)
    plane = lax.axis_index("lz")
    near_ids = jnp.arange(near, dtype=jnp.int32)
    near_experts = (near_ids // rows_of) * (planes * rows_of) + plane * rows_of + near_ids % rows_of
    hit = seen_routes[..., None] == near_experts
    named = jnp.any(hit, axis=2)
    earlier = (
        jnp.arange(tokens_dev)[:, None] > jnp.arange(tokens_dev)[None, :]
    ).astype(jnp.bfloat16)
    rank = jnp.einsum(
        "ts,zsj->jzt", earlier, named.astype(jnp.bfloat16), preferred_element_type=jnp.float32
    ).astype(jnp.int32)
    choose = jnp.transpose(named, (2, 0, 1))[:, :, None, :] & (
        rank[:, :, None, :] == jnp.arange(capacity, dtype=jnp.int32)[None, None, :, None]
    )
    choose_b = choose.astype(jnp.bfloat16)
    gate_tj = jnp.sum(
        jnp.where(hit, seen_gates[..., None], jnp.zeros((), jnp.bfloat16)), axis=2
    )
    send_gate = jnp.sum(
        jnp.where(
            choose, jnp.transpose(gate_tj, (2, 0, 1))[:, :, None, :], jnp.zeros((), jnp.bfloat16)
        ),
        axis=3,
    )
    gate_block = (
        jnp.zeros((near, planes, capacity, pad), jnp.bfloat16).at[..., 0].set(send_gate)
    )
    send_x = jnp.einsum(
        "jzrt,ztd->jzrd", choose_b, seen_x[:, :, :width], preferred_element_type=jnp.float32
    ).astype(jnp.bfloat16)
    send_x = jnp.concatenate([send_x, gate_block], axis=3).reshape(
        near, planes * capacity, width + pad
    )
    send_dy = (
        jnp.einsum("jzrt,ztd->jzrd", choose_b, seen_dy, preferred_element_type=jnp.float32)
        .astype(jnp.bfloat16)
        .reshape(near, planes * capacity, width)
    )
    all_weights = lax.all_gather(
        jnp.concatenate([w_gate, w_up, w_down], axis=2), "dp", axis=1, tiled=True
    )[0]
    gate_proj = all_weights[:, :hidden_units]
    up_proj = all_weights[:, hidden_units : 2 * hidden_units]
    down_proj = all_weights[:, 2 * hidden_units :]
    recv_x = lax.all_to_all(send_x, ("node", "ly"), split_axis=0, concat_axis=0, tiled=True)
    recv_dy = lax.all_to_all(send_dy, ("node", "ly"), split_axis=0, concat_axis=0, tiled=True)
    flat_x = recv_x.reshape(slots, width + pad)
    results = expert_rows(
        flat_x[:, :width],
        recv_dy.reshape(slots, width),
        flat_x[:, width],
        gate_proj,
        up_proj,
        down_proj,
    )
    grad_block = jnp.zeros((slots, pad), jnp.bfloat16).at[:, 0].set(results[1])
    back_lo = jnp.concatenate([results[0][:, :half], grad_block], axis=1).reshape(
        near, planes * capacity, half + pad
    )
    back_hi = results[0][:, half:].reshape(near, planes * capacity, width - half)
    home_lo = lax.all_to_all(
        back_lo, ("node", "ly"), split_axis=0, concat_axis=0, tiled=True
    ).reshape(near, planes, capacity, half + pad)
    home_hi = lax.all_to_all(
        back_hi, ("node", "ly"), split_axis=0, concat_axis=0, tiled=True
    ).reshape(near, planes, capacity, width - half)
    partial_lo = jnp.einsum(
        "jzrt,jzrd->ztd", choose_b, home_lo[..., :half], preferred_element_type=jnp.float32
    )
    gate_jzt = jnp.sum(
        jnp.where(choose, home_lo[..., half][..., None], jnp.zeros((), jnp.bfloat16)), axis=2
    )
    pick_gate = jnp.sum(
        jnp.where(
            hit, jnp.transpose(gate_jzt, (1, 2, 0))[:, :, None, :], jnp.zeros((), jnp.bfloat16)
        ),
        axis=3,
    )
    gate_cols = (
        jnp.zeros((planes, tokens_dev, pad), jnp.float32)
        .at[..., :top_count]
        .set(pick_gate.astype(jnp.float32))
    )
    reduced_lo = lax.psum_scatter(
        jnp.concatenate([partial_lo, gate_cols], axis=2), "lz", scatter_dimension=0, tiled=True
    )[0]
    partial_hi = jnp.einsum(
        "jzrt,jzrd->ztd", choose_b, home_hi, preferred_element_type=jnp.float32
    )
    reduced_hi = lax.psum_scatter(partial_hi, "lz", scatter_dimension=0, tiled=True)[0]
    input_grad = jnp.concatenate(
        [reduced_lo[:, :half], reduced_hi], axis=1
    ).astype(jnp.bfloat16)
    gate_grad = reduced_lo[:, half : half + top_count].astype(jnp.bfloat16)
    summed = ring_sum_scatter(jnp.concatenate([results[2], results[3], results[4]], axis=1))
    return (
        input_grad,
        gate_grad,
        summed[None, :, :hidden_units],
        summed[None, :, hidden_units : 2 * hidden_units],
        summed[None, :, 2 * hidden_units :],
    )


def solution(mesh):
    local_size = mesh.shape["local"]
    rows_of = 4 if local_size % 4 == 0 else 1
    split = jax.sharding.Mesh(
        mesh.devices.reshape(
            mesh.shape["dp"], mesh.shape["node"], local_size // rows_of, rows_of
        ),
        ("dp", "node", "lz", "ly"),
    )
    rows = P(("dp", "node", "lz", "ly"), None)
    expert = P(("node", "lz", "ly"), "dp", None)
    return jax.shard_map(
        local,
        mesh=split,
        in_specs=(rows, rows, rows, rows, expert, expert, expert),
        out_specs=(rows, rows, expert, expert, expert),
        check_vma=False,
    )
```

```python
import jax
import jax.numpy as jnp
from jax import lax
from jax.sharding import PartitionSpec as P


def expert_rows(rows_x, rows_dy, rows_gate, gate_proj, up_proj, down_proj):
    pre_gate = jnp.dot(rows_x, gate_proj, preferred_element_type=jnp.float32)
    pre_up = jnp.dot(rows_x, up_proj, preferred_element_type=jnp.float32)
    gate_sigmoid = jax.nn.sigmoid(pre_gate)
    activated = pre_gate * gate_sigmoid
    hidden = activated * pre_up
    upstream = jnp.dot(rows_dy, down_proj, preferred_element_type=jnp.float32)
    gate_grad = jnp.sum(upstream * hidden, axis=1).astype(jnp.bfloat16)
    weight = rows_gate.astype(jnp.float32)[:, None]
    scaled_hidden = (weight * hidden).astype(jnp.bfloat16)
    hidden_grad = weight * upstream
    pre_gate_grad = (
        hidden_grad * pre_up * gate_sigmoid * (1.0 + pre_gate * (1.0 - gate_sigmoid))
    ).astype(jnp.bfloat16)
    pre_up_grad = (hidden_grad * activated).astype(jnp.bfloat16)
    over_rows = (((0,), (0,)), ((), ()))
    down_grad = lax.dot_general(
        rows_dy, scaled_hidden, over_rows, preferred_element_type=jnp.float32
    )
    gate_wgrad = lax.dot_general(
        rows_x, pre_gate_grad, over_rows, preferred_element_type=jnp.float32
    )
    up_wgrad = lax.dot_general(rows_x, pre_up_grad, over_rows, preferred_element_type=jnp.float32)
    over_hidden = (((1,), (1,)), ((), ()))
    input_rows = lax.dot_general(
        pre_gate_grad, gate_proj, over_hidden, preferred_element_type=jnp.float32
    )
    input_rows = input_rows + lax.dot_general(
        pre_up_grad, up_proj, over_hidden, preferred_element_type=jnp.float32
    )
    return (input_rows.astype(jnp.bfloat16), gate_grad, gate_wgrad, up_wgrad, down_grad)


def local(tokens, cotangent, routes, gates, w_gate, w_up, w_down):
    tokens_dev, top_count = routes.shape
    width = tokens.shape[1]
    hidden_units = w_gate.shape[2]
    cores = lax.axis_size("node")
    planes = lax.axis_size("lz")
    rows_of = lax.axis_size("ly")
    experts = cores * planes * rows_of
    capacity = min(
        tokens_dev,
        max(3 * tokens_dev * top_count // (2 * experts), tokens_dev * top_count // experts),
    )
    near = cores * rows_of
    slots = near * planes * capacity
    half = width // 2
    meta = jnp.concatenate([gates, routes.astype(jnp.bfloat16)], axis=1).reshape(1, -1)
    meta = jnp.pad(meta, ((0, 0), (0, width - meta.shape[1])))
    seen_x = lax.all_gather(jnp.concatenate([tokens, meta], axis=0), "lz", axis=0, tiled=False)
    seen_dy = lax.all_gather(cotangent, "lz", axis=0, tiled=False)
    seen_meta = seen_x[:, tokens_dev, : 2 * tokens_dev * top_count].reshape(
        planes, tokens_dev, 2 * top_count
    )
    seen_gates = seen_meta[..., :top_count]
    seen_routes = seen_meta[..., top_count:].astype(jnp.int32)
    plane = lax.axis_index("lz")
    near_ids = jnp.arange(near, dtype=jnp.int32)
    near_experts = (near_ids // rows_of) * (planes * rows_of) + plane * rows_of + near_ids % rows_of
    hit = seen_routes[..., None] == near_experts
    named = jnp.any(hit, axis=2)
    earlier = (
        jnp.arange(tokens_dev)[:, None] > jnp.arange(tokens_dev)[None, :]
    ).astype(jnp.bfloat16)
    rank = jnp.einsum(
        "ts,zsj->jzt", earlier, named.astype(jnp.bfloat16), preferred_element_type=jnp.float32
    ).astype(jnp.int32)
    choose = jnp.transpose(named, (2, 0, 1))[:, :, None, :] & (
        rank[:, :, None, :] == jnp.arange(capacity, dtype=jnp.int32)[None, None, :, None]
    )
    choose_b = choose.astype(jnp.bfloat16)
    gate_tj = jnp.sum(
        jnp.where(hit, seen_gates[..., None], jnp.zeros((), jnp.bfloat16)), axis=2
    )
    send_gate = jnp.sum(
        jnp.where(
            choose, jnp.transpose(gate_tj, (2, 0, 1))[:, :, None, :], jnp.zeros((), jnp.bfloat16)
        ),
        axis=3,
    )
    gate_row = jnp.pad(
        send_gate.reshape(near, 1, planes * capacity),
        ((0, 0), (0, 0), (0, width - planes * capacity)),
    )
    send_x = jnp.einsum(
        "jzrt,ztd->jzrd",
        choose_b,
        seen_x[:, :tokens_dev, :],
        preferred_element_type=jnp.float32,
    ).astype(jnp.bfloat16)
    send_x = jnp.concatenate(
        [send_x.reshape(near, planes * capacity, width), gate_row], axis=1
    )
    send_dy = (
        jnp.einsum("jzrt,ztd->jzrd", choose_b, seen_dy, preferred_element_type=jnp.float32)
        .astype(jnp.bfloat16)
        .reshape(near, planes * capacity, width)
    )
    all_weights = lax.all_gather(
        jnp.concatenate([w_gate, w_up, w_down], axis=2), "dp", axis=1, tiled=True
    )[0]
    gate_proj = all_weights[:, :hidden_units]
    up_proj = all_weights[:, hidden_units : 2 * hidden_units]
    down_proj = all_weights[:, 2 * hidden_units :]
    recv_x = lax.all_to_all(send_x, ("node", "ly"), split_axis=0, concat_axis=0, tiled=True)
    recv_dy = lax.all_to_all(send_dy, ("node", "ly"), split_axis=0, concat_axis=0, tiled=True)
    results = expert_rows(
        recv_x[:, : planes * capacity, :].reshape(slots, width),
        recv_dy.reshape(slots, width),
        recv_x[:, planes * capacity, : planes * capacity].reshape(slots),
        gate_proj,
        up_proj,
        down_proj,
    )
    grad_row = jnp.pad(
        results[1].reshape(near, 1, planes * capacity),
        ((0, 0), (0, 0), (0, half - planes * capacity)),
    )
    back_lo = jnp.concatenate(
        [results[0][:, :half].reshape(near, planes * capacity, half), grad_row], axis=1
    )
    back_hi = results[0][:, half:].reshape(near, planes * capacity, width - half)
    home_lo = lax.all_to_all(back_lo, ("node", "ly"), split_axis=0, concat_axis=0, tiled=True)
    home_gate = home_lo[:, planes * capacity, : planes * capacity].reshape(
        near, planes, capacity
    )
    home_lo = home_lo[:, : planes * capacity, :].reshape(near, planes, capacity, half)
    home_hi = lax.all_to_all(
        back_hi, ("node", "ly"), split_axis=0, concat_axis=0, tiled=True
    ).reshape(near, planes, capacity, width - half)
    partial_lo = jnp.einsum(
        "jzrt,jzrd->ztd", choose_b, home_lo, preferred_element_type=jnp.float32
    )
    gate_jzt = jnp.sum(
        jnp.where(choose, home_gate[..., None], jnp.zeros((), jnp.bfloat16)), axis=2
    )
    pick_gate = jnp.sum(
        jnp.where(
            hit, jnp.transpose(gate_jzt, (1, 2, 0))[:, :, None, :], jnp.zeros((), jnp.bfloat16)
        ),
        axis=3,
    )
    gate_cols = jnp.pad(
        pick_gate.astype(jnp.float32).reshape(planes, 1, tokens_dev * top_count),
        ((0, 0), (0, 0), (0, half - tokens_dev * top_count)),
    )
    summed = lax.psum_scatter(
        jnp.concatenate([results[2], results[3], results[4]], axis=1),
        "dp",
        scatter_dimension=0,
        tiled=True,
    )
    summed, partial_lo, gate_cols = lax.optimization_barrier((summed, partial_lo, gate_cols))
    reduced_lo = lax.psum_scatter(
        jnp.concatenate([partial_lo, gate_cols], axis=1), "lz", scatter_dimension=0, tiled=True
    )[0]
    partial_hi = jnp.einsum(
        "jzrt,jzrd->ztd", choose_b, home_hi, preferred_element_type=jnp.float32
    )
    reduced_hi = lax.psum_scatter(partial_hi, "lz", scatter_dimension=0, tiled=True)[0]
    input_grad = jnp.concatenate(
        [reduced_lo[:tokens_dev], reduced_hi], axis=1
    ).astype(jnp.bfloat16)
    gate_grad = (
        reduced_lo[tokens_dev, : tokens_dev * top_count]
        .reshape(tokens_dev, top_count)
        .astype(jnp.bfloat16)
    )
    return (
        input_grad,
        gate_grad,
        summed[None, :, :hidden_units],
        summed[None, :, hidden_units : 2 * hidden_units],
        summed[None, :, 2 * hidden_units :],
    )


def solution(mesh):
    local_size = mesh.shape["local"]
    rows_of = 4 if local_size % 4 == 0 else 1
    split = jax.sharding.Mesh(
        mesh.devices.reshape(
            mesh.shape["dp"], mesh.shape["node"], local_size // rows_of, rows_of
        ),
        ("dp", "node", "lz", "ly"),
    )
    rows = P(("dp", "node", "lz", "ly"), None)
    expert = P(("node", "lz", "ly"), "dp", None)
    return jax.shard_map(
        local,
        mesh=split,
        in_specs=(rows, rows, rows, rows, expert, expert, expert),
        out_specs=(rows, rows, expert, expert, expert),
        check_vma=False,
    )
```

```python
import jax
import jax.numpy as jnp
from jax import lax
from jax.sharding import PartitionSpec as P


def expert_rows(rows_x, rows_dy, rows_gate, gate_proj, up_proj, down_proj):
    pre_gate = jnp.dot(rows_x, gate_proj, preferred_element_type=jnp.float32)
    pre_up = jnp.dot(rows_x, up_proj, preferred_element_type=jnp.float32)
    gate_sigmoid = jax.nn.sigmoid(pre_gate)
    activated = pre_gate * gate_sigmoid
    hidden = activated * pre_up
    upstream = jnp.dot(rows_dy, down_proj, preferred_element_type=jnp.float32)
    gate_grad = jnp.sum(upstream * hidden, axis=1).astype(jnp.bfloat16)
    weight = rows_gate.astype(jnp.float32)[:, None]
    scaled_hidden = (weight * hidden).astype(jnp.bfloat16)
    hidden_grad = weight * upstream
    pre_gate_grad = (
        hidden_grad * pre_up * gate_sigmoid * (1.0 + pre_gate * (1.0 - gate_sigmoid))
    ).astype(jnp.bfloat16)
    pre_up_grad = (hidden_grad * activated).astype(jnp.bfloat16)
    over_rows = (((0,), (0,)), ((), ()))
    down_grad = lax.dot_general(
        rows_dy, scaled_hidden, over_rows, preferred_element_type=jnp.float32
    )
    gate_wgrad = lax.dot_general(
        rows_x, pre_gate_grad, over_rows, preferred_element_type=jnp.float32
    )
    up_wgrad = lax.dot_general(rows_x, pre_up_grad, over_rows, preferred_element_type=jnp.float32)
    over_hidden = (((1,), (1,)), ((), ()))
    input_rows = lax.dot_general(
        pre_gate_grad, gate_proj, over_hidden, preferred_element_type=jnp.float32
    )
    input_rows = input_rows + lax.dot_general(
        pre_up_grad, up_proj, over_hidden, preferred_element_type=jnp.float32
    )
    return (input_rows.astype(jnp.bfloat16), gate_grad, gate_wgrad, up_wgrad, down_grad)


def local(tokens, cotangent, routes, gates, w_gate, w_up, w_down):
    tokens_dev, top_count = routes.shape
    width = tokens.shape[1]
    hidden_units = w_gate.shape[2]
    cores = lax.axis_size("node")
    planes = lax.axis_size("lz")
    rows_of = lax.axis_size("ly")
    experts = cores * planes * rows_of
    capacity = min(
        tokens_dev,
        max(3 * tokens_dev * top_count // (2 * experts), tokens_dev * top_count // experts),
    )
    near = cores * rows_of
    slots = near * planes * capacity
    half = width // 2
    meta = jnp.concatenate([gates, routes.astype(jnp.bfloat16)], axis=1).reshape(1, -1)
    meta = jnp.pad(meta, ((0, 0), (0, width - meta.shape[1])))
    seen_x = lax.all_gather(jnp.concatenate([tokens, meta], axis=0), "lz", axis=0, tiled=False)
    seen_dy = lax.all_gather(cotangent, "lz", axis=0, tiled=False)
    seen_meta = seen_x[:, tokens_dev, : 2 * tokens_dev * top_count].reshape(
        planes, tokens_dev, 2 * top_count
    )
    seen_gates = seen_meta[..., :top_count]
    seen_routes = seen_meta[..., top_count:].astype(jnp.int32)
    plane = lax.axis_index("lz")
    near_ids = jnp.arange(near, dtype=jnp.int32)
    near_experts = (near_ids // rows_of) * (planes * rows_of) + plane * rows_of + near_ids % rows_of
    hit = seen_routes[..., None] == near_experts
    named = jnp.any(hit, axis=2)
    earlier = (
        jnp.arange(tokens_dev)[:, None] > jnp.arange(tokens_dev)[None, :]
    ).astype(jnp.bfloat16)
    rank = jnp.einsum(
        "ts,zsj->jzt", earlier, named.astype(jnp.bfloat16), preferred_element_type=jnp.float32
    ).astype(jnp.int32)
    choose = jnp.transpose(named, (2, 0, 1))[:, :, None, :] & (
        rank[:, :, None, :] == jnp.arange(capacity, dtype=jnp.int32)[None, None, :, None]
    )
    choose_b = choose.astype(jnp.bfloat16)
    gate_tj = jnp.sum(
        jnp.where(hit, seen_gates[..., None], jnp.zeros((), jnp.bfloat16)), axis=2
    )
    send_gate = jnp.sum(
        jnp.where(
            choose, jnp.transpose(gate_tj, (2, 0, 1))[:, :, None, :], jnp.zeros((), jnp.bfloat16)
        ),
        axis=3,
    )
    gate_row = jnp.pad(
        send_gate.reshape(near, 1, planes * capacity),
        ((0, 0), (0, 0), (0, width - planes * capacity)),
    )
    send_x = jnp.einsum(
        "jzrt,ztd->jzrd",
        choose_b,
        seen_x[:, :tokens_dev, :],
        preferred_element_type=jnp.float32,
    ).astype(jnp.bfloat16)
    send_x = jnp.concatenate(
        [send_x.reshape(near, planes * capacity, width), gate_row], axis=1
    )
    send_dy = (
        jnp.einsum("jzrt,ztd->jzrd", choose_b, seen_dy, preferred_element_type=jnp.float32)
        .astype(jnp.bfloat16)
        .reshape(near, planes * capacity, width)
    )
    all_weights = lax.all_gather(
        jnp.concatenate([w_gate, w_up, w_down], axis=2), "dp", axis=1, tiled=True
    )[0]
    gate_proj = all_weights[:, :hidden_units]
    up_proj = all_weights[:, hidden_units : 2 * hidden_units]
    down_proj = all_weights[:, 2 * hidden_units :]
    recv_x = lax.all_to_all(send_x, ("node", "ly"), split_axis=0, concat_axis=0, tiled=True)
    recv_dy = lax.all_to_all(send_dy, ("node", "ly"), split_axis=0, concat_axis=0, tiled=True)
    results = expert_rows(
        recv_x[:, : planes * capacity, :].reshape(slots, width),
        recv_dy.reshape(slots, width),
        recv_x[:, planes * capacity, : planes * capacity].reshape(slots),
        gate_proj,
        up_proj,
        down_proj,
    )
    grad_row = jnp.pad(
        results[1].reshape(near, 1, planes * capacity),
        ((0, 0), (0, 0), (0, half - planes * capacity)),
    )
    back_lo = jnp.concatenate(
        [results[0][:, :half].reshape(near, planes * capacity, half), grad_row], axis=1
    )
    back_hi = results[0][:, half:].reshape(near, planes * capacity, width - half)
    home_lo = lax.all_to_all(back_lo, ("node", "ly"), split_axis=0, concat_axis=0, tiled=True)
    home_gate = home_lo[:, planes * capacity, : planes * capacity].reshape(
        near, planes, capacity
    )
    home_lo = home_lo[:, : planes * capacity, :].reshape(near, planes, capacity, half)
    home_hi = lax.all_to_all(
        back_hi, ("node", "ly"), split_axis=0, concat_axis=0, tiled=True
    ).reshape(near, planes, capacity, width - half)
    partial_lo = jnp.einsum(
        "jzrt,jzrd->ztd", choose_b, home_lo, preferred_element_type=jnp.float32
    )
    gate_jzt = jnp.sum(
        jnp.where(choose, home_gate[..., None], jnp.zeros((), jnp.bfloat16)), axis=2
    )
    pick_gate = jnp.sum(
        jnp.where(
            hit, jnp.transpose(gate_jzt, (1, 2, 0))[:, :, None, :], jnp.zeros((), jnp.bfloat16)
        ),
        axis=3,
    )
    gate_cols = jnp.pad(
        pick_gate.astype(jnp.float32).reshape(planes, 1, tokens_dev * top_count),
        ((0, 0), (0, 0), (0, half - tokens_dev * top_count)),
    )
    summed_down = lax.psum_scatter(results[4], "dp", scatter_dimension=0, tiled=True)
    summed = lax.psum_scatter(
        jnp.concatenate([results[2], results[3]], axis=1), "dp", scatter_dimension=0, tiled=True
    )
    summed_down, summed, partial_lo, gate_cols = lax.optimization_barrier(
        (summed_down, summed, partial_lo, gate_cols)
    )
    reduced_lo = lax.psum_scatter(
        jnp.concatenate([partial_lo, gate_cols], axis=1), "lz", scatter_dimension=0, tiled=True
    )[0]
    partial_hi = jnp.einsum(
        "jzrt,jzrd->ztd", choose_b, home_hi, preferred_element_type=jnp.float32
    )
    reduced_hi = lax.psum_scatter(partial_hi, "lz", scatter_dimension=0, tiled=True)[0]
    input_grad = jnp.concatenate(
        [reduced_lo[:tokens_dev], reduced_hi], axis=1
    ).astype(jnp.bfloat16)
    gate_grad = (
        reduced_lo[tokens_dev, : tokens_dev * top_count]
        .reshape(tokens_dev, top_count)
        .astype(jnp.bfloat16)
    )
    return (
        input_grad,
        gate_grad,
        summed[None, :, :hidden_units],
        summed[None, :, hidden_units : 2 * hidden_units],
        summed_down[None],
    )


def solution(mesh):
    local_size = mesh.shape["local"]
    rows_of = 4 if local_size % 4 == 0 else 1
    split = jax.sharding.Mesh(
        mesh.devices.reshape(
            mesh.shape["dp"], mesh.shape["node"], local_size // rows_of, rows_of
        ),
        ("dp", "node", "lz", "ly"),
    )
    rows = P(("dp", "node", "lz", "ly"), None)
    expert = P(("node", "lz", "ly"), "dp", None)
    return jax.shard_map(
        local,
        mesh=split,
        in_specs=(rows, rows, rows, rows, expert, expert, expert),
        out_specs=(rows, rows, expert, expert, expert),
        check_vma=False,
    )
```

```python
import jax
import jax.numpy as jnp
from jax import lax
from jax.sharding import PartitionSpec as P


def expert_rows(rows_x, rows_dy, rows_gate, gate_proj, up_proj, down_proj):
    pre_gate = jnp.dot(rows_x, gate_proj, preferred_element_type=jnp.float32)
    pre_up = jnp.dot(rows_x, up_proj, preferred_element_type=jnp.float32)
    gate_sigmoid = jax.nn.sigmoid(pre_gate)
    activated = pre_gate * gate_sigmoid
    hidden = activated * pre_up
    upstream = jnp.dot(rows_dy, down_proj, preferred_element_type=jnp.float32)
    gate_grad = jnp.sum(upstream * hidden, axis=1).astype(jnp.bfloat16)
    weight = rows_gate.astype(jnp.float32)[:, None]
    scaled_hidden = (weight * hidden).astype(jnp.bfloat16)
    hidden_grad = weight * upstream
    pre_gate_grad = (
        hidden_grad * pre_up * gate_sigmoid * (1.0 + pre_gate * (1.0 - gate_sigmoid))
    ).astype(jnp.bfloat16)
    pre_up_grad = (hidden_grad * activated).astype(jnp.bfloat16)
    over_rows = (((0,), (0,)), ((), ()))
    down_grad = lax.dot_general(
        rows_dy, scaled_hidden, over_rows, preferred_element_type=jnp.float32
    )
    gate_wgrad = lax.dot_general(
        rows_x, pre_gate_grad, over_rows, preferred_element_type=jnp.float32
    )
    up_wgrad = lax.dot_general(rows_x, pre_up_grad, over_rows, preferred_element_type=jnp.float32)
    over_hidden = (((1,), (1,)), ((), ()))
    input_rows = lax.dot_general(
        pre_gate_grad, gate_proj, over_hidden, preferred_element_type=jnp.float32
    )
    input_rows = input_rows + lax.dot_general(
        pre_up_grad, up_proj, over_hidden, preferred_element_type=jnp.float32
    )
    return (input_rows.astype(jnp.bfloat16), gate_grad, gate_wgrad, up_wgrad, down_grad)


def local(tokens, cotangent, routes, gates, w_gate, w_up, w_down):
    tokens_dev, top_count = routes.shape
    width = tokens.shape[1]
    hidden_units = w_gate.shape[2]
    cores = lax.axis_size("node")
    planes = lax.axis_size("lz")
    rows_of = lax.axis_size("ly")
    experts = cores * planes * rows_of
    capacity = min(
        tokens_dev,
        max(3 * tokens_dev * top_count // (2 * experts), tokens_dev * top_count // experts),
    )
    near = cores * rows_of
    slots = near * planes * capacity
    half = width // 2
    meta = jnp.concatenate([gates, routes.astype(jnp.bfloat16)], axis=1).reshape(1, -1)
    meta = jnp.pad(meta, ((0, 0), (0, width - meta.shape[1])))
    seen_x = lax.all_gather(jnp.concatenate([tokens, meta], axis=0), "lz", axis=0, tiled=False)
    seen_dy = lax.all_gather(cotangent, "lz", axis=0, tiled=False)
    seen_meta = seen_x[:, tokens_dev, : 2 * tokens_dev * top_count].reshape(
        planes, tokens_dev, 2 * top_count
    )
    seen_gates = seen_meta[..., :top_count]
    seen_routes = seen_meta[..., top_count:].astype(jnp.int32)
    plane = lax.axis_index("lz")
    near_ids = jnp.arange(near, dtype=jnp.int32)
    near_experts = (near_ids // rows_of) * (planes * rows_of) + plane * rows_of + near_ids % rows_of
    hit = seen_routes[..., None] == near_experts
    named = jnp.any(hit, axis=2)
    earlier = (
        jnp.arange(tokens_dev)[:, None] > jnp.arange(tokens_dev)[None, :]
    ).astype(jnp.bfloat16)
    rank = jnp.einsum(
        "ts,zsj->jzt", earlier, named.astype(jnp.bfloat16), preferred_element_type=jnp.float32
    ).astype(jnp.int32)
    choose = jnp.transpose(named, (2, 0, 1))[:, :, None, :] & (
        rank[:, :, None, :] == jnp.arange(capacity, dtype=jnp.int32)[None, None, :, None]
    )
    choose_b = choose.astype(jnp.bfloat16)
    gate_tj = jnp.sum(
        jnp.where(hit, seen_gates[..., None], jnp.zeros((), jnp.bfloat16)), axis=2
    )
    send_gate = jnp.sum(
        jnp.where(
            choose, jnp.transpose(gate_tj, (2, 0, 1))[:, :, None, :], jnp.zeros((), jnp.bfloat16)
        ),
        axis=3,
    )
    gate_row = jnp.pad(
        send_gate.reshape(near, 1, planes * capacity),
        ((0, 0), (0, 0), (0, width - planes * capacity)),
    )
    send_x = jnp.einsum(
        "jzrt,ztd->jzrd",
        choose_b,
        seen_x[:, :tokens_dev, :],
        preferred_element_type=jnp.float32,
    ).astype(jnp.bfloat16)
    send_x = send_x.reshape(near, planes * capacity, width)
    send_dy = (
        jnp.einsum("jzrt,ztd->jzrd", choose_b, seen_dy, preferred_element_type=jnp.float32)
        .astype(jnp.bfloat16)
        .reshape(near, planes * capacity, width)
    )
    send_dy = jnp.concatenate([send_dy, gate_row], axis=1)
    all_weights = lax.all_gather(
        jnp.concatenate([w_gate, w_up, w_down], axis=2), "dp", axis=1, tiled=True
    )[0]
    gate_proj = all_weights[:, :hidden_units]
    up_proj = all_weights[:, hidden_units : 2 * hidden_units]
    down_proj = all_weights[:, 2 * hidden_units :]
    recv_x = lax.all_to_all(send_x, ("node", "ly"), split_axis=0, concat_axis=0, tiled=True)
    recv_dy = lax.all_to_all(send_dy, ("node", "ly"), split_axis=0, concat_axis=0, tiled=True)
    results = expert_rows(
        recv_x.reshape(slots, width),
        recv_dy[:, : planes * capacity, :].reshape(slots, width),
        recv_dy[:, planes * capacity, : planes * capacity].reshape(slots),
        gate_proj,
        up_proj,
        down_proj,
    )
    grad_row = jnp.pad(
        results[1].reshape(near, 1, planes * capacity),
        ((0, 0), (0, 0), (0, half - planes * capacity)),
    )
    back_lo = jnp.concatenate(
        [results[0][:, :half].reshape(near, planes * capacity, half), grad_row], axis=1
    )
    back_hi = results[0][:, half:].reshape(near, planes * capacity, width - half)
    home_lo = lax.all_to_all(back_lo, ("node", "ly"), split_axis=0, concat_axis=0, tiled=True)
    home_gate = home_lo[:, planes * capacity, : planes * capacity].reshape(
        near, planes, capacity
    )
    home_lo = home_lo[:, : planes * capacity, :].reshape(near, planes, capacity, half)
    home_hi = lax.all_to_all(
        back_hi, ("node", "ly"), split_axis=0, concat_axis=0, tiled=True
    ).reshape(near, planes, capacity, width - half)
    partial_lo = jnp.einsum(
        "jzrt,jzrd->ztd", choose_b, home_lo, preferred_element_type=jnp.float32
    )
    gate_jzt = jnp.sum(
        jnp.where(choose, home_gate[..., None], jnp.zeros((), jnp.bfloat16)), axis=2
    )
    pick_gate = jnp.sum(
        jnp.where(
            hit, jnp.transpose(gate_jzt, (1, 2, 0))[:, :, None, :], jnp.zeros((), jnp.bfloat16)
        ),
        axis=3,
    )
    gate_cols = jnp.pad(
        pick_gate.astype(jnp.float32).reshape(planes, 1, tokens_dev * top_count),
        ((0, 0), (0, 0), (0, half - tokens_dev * top_count)),
    )
    summed_down = lax.psum_scatter(results[4], "dp", scatter_dimension=0, tiled=True)
    summed = lax.psum_scatter(
        jnp.concatenate([results[2], results[3]], axis=1), "dp", scatter_dimension=0, tiled=True
    )
    summed_down, summed, partial_lo, gate_cols = lax.optimization_barrier(
        (summed_down, summed, partial_lo, gate_cols)
    )
    reduced_lo = lax.psum_scatter(
        jnp.concatenate([partial_lo, gate_cols], axis=1), "lz", scatter_dimension=0, tiled=True
    )[0]
    partial_hi = jnp.einsum(
        "jzrt,jzrd->ztd", choose_b, home_hi, preferred_element_type=jnp.float32
    )
    reduced_hi = lax.psum_scatter(partial_hi, "lz", scatter_dimension=0, tiled=True)[0]
    input_grad = jnp.concatenate(
        [reduced_lo[:tokens_dev], reduced_hi], axis=1
    ).astype(jnp.bfloat16)
    gate_grad = (
        reduced_lo[tokens_dev, : tokens_dev * top_count]
        .reshape(tokens_dev, top_count)
        .astype(jnp.bfloat16)
    )
    return (
        input_grad,
        gate_grad,
        summed[None, :, :hidden_units],
        summed[None, :, hidden_units : 2 * hidden_units],
        summed_down[None],
    )


def solution(mesh):
    local_size = mesh.shape["local"]
    rows_of = 4 if local_size % 4 == 0 else 1
    split = jax.sharding.Mesh(
        mesh.devices.reshape(
            mesh.shape["dp"], mesh.shape["node"], local_size // rows_of, rows_of
        ),
        ("dp", "node", "lz", "ly"),
    )
    rows = P(("dp", "node", "lz", "ly"), None)
    expert = P(("node", "lz", "ly"), "dp", None)
    return jax.shard_map(
        local,
        mesh=split,
        in_specs=(rows, rows, rows, rows, expert, expert, expert),
        out_specs=(rows, rows, expert, expert, expert),
        check_vma=False,
    )
```

```python
import jax
import jax.numpy as jnp
from jax import lax
from jax.sharding import PartitionSpec as P


def expert_rows(rows_x, rows_dy, rows_gate, gate_proj, up_proj, down_proj):
    pre_gate = jnp.dot(rows_x, gate_proj, preferred_element_type=jnp.float32)
    pre_up = jnp.dot(rows_x, up_proj, preferred_element_type=jnp.float32)
    gate_sigmoid = jax.nn.sigmoid(pre_gate)
    activated = pre_gate * gate_sigmoid
    hidden = activated * pre_up
    upstream = jnp.dot(rows_dy, down_proj, preferred_element_type=jnp.float32)
    gate_grad = jnp.sum(upstream * hidden, axis=1).astype(jnp.bfloat16)
    weight = rows_gate.astype(jnp.float32)[:, None]
    scaled_hidden = (weight * hidden).astype(jnp.bfloat16)
    hidden_grad = weight * upstream
    pre_gate_grad = (
        hidden_grad * pre_up * gate_sigmoid * (1.0 + pre_gate * (1.0 - gate_sigmoid))
    ).astype(jnp.bfloat16)
    pre_up_grad = (hidden_grad * activated).astype(jnp.bfloat16)
    over_rows = (((0,), (0,)), ((), ()))
    down_grad = lax.dot_general(
        rows_dy, scaled_hidden, over_rows, preferred_element_type=jnp.float32
    )
    gate_wgrad = lax.dot_general(
        rows_x, pre_gate_grad, over_rows, preferred_element_type=jnp.float32
    )
    up_wgrad = lax.dot_general(rows_x, pre_up_grad, over_rows, preferred_element_type=jnp.float32)
    over_hidden = (((1,), (1,)), ((), ()))
    input_rows = lax.dot_general(
        pre_gate_grad, gate_proj, over_hidden, preferred_element_type=jnp.float32
    )
    input_rows = input_rows + lax.dot_general(
        pre_up_grad, up_proj, over_hidden, preferred_element_type=jnp.float32
    )
    return (input_rows.astype(jnp.bfloat16), gate_grad, gate_wgrad, up_wgrad, down_grad)


def local(tokens, cotangent, routes, gates, w_gate, w_up, w_down):
    tokens_dev, top_count = routes.shape
    width = tokens.shape[1]
    hidden_units = w_gate.shape[2]
    cores = lax.axis_size("node")
    planes = lax.axis_size("lz")
    rows_of = lax.axis_size("ly")
    experts = cores * planes * rows_of
    capacity = min(
        tokens_dev,
        max(3 * tokens_dev * top_count // (2 * experts), tokens_dev * top_count // experts),
    )
    near = cores * rows_of
    slots = near * planes * capacity
    half = width // 2
    meta = jnp.concatenate([gates, routes.astype(jnp.bfloat16)], axis=1).reshape(1, -1)
    meta = jnp.pad(meta, ((0, 0), (0, width - meta.shape[1])))
    seen_row = lax.all_gather(meta, "lz", axis=0, tiled=False)
    seen_x = lax.all_gather(tokens, "lz", axis=0, tiled=False)
    seen_dy = lax.all_gather(cotangent, "lz", axis=0, tiled=False)
    seen_meta = seen_row[:, 0, : 2 * tokens_dev * top_count].reshape(
        planes, tokens_dev, 2 * top_count
    )
    seen_gates = seen_meta[..., :top_count]
    seen_routes = seen_meta[..., top_count:].astype(jnp.int32)
    plane = lax.axis_index("lz")
    near_ids = jnp.arange(near, dtype=jnp.int32)
    near_experts = (near_ids // rows_of) * (planes * rows_of) + plane * rows_of + near_ids % rows_of
    hit = seen_routes[..., None] == near_experts
    named = jnp.any(hit, axis=2)
    earlier = (
        jnp.arange(tokens_dev)[:, None] > jnp.arange(tokens_dev)[None, :]
    ).astype(jnp.bfloat16)
    rank = jnp.einsum(
        "ts,zsj->jzt", earlier, named.astype(jnp.bfloat16), preferred_element_type=jnp.float32
    ).astype(jnp.int32)
    choose = jnp.transpose(named, (2, 0, 1))[:, :, None, :] & (
        rank[:, :, None, :] == jnp.arange(capacity, dtype=jnp.int32)[None, None, :, None]
    )
    choose_b = choose.astype(jnp.bfloat16)
    gate_tj = jnp.sum(
        jnp.where(hit, seen_gates[..., None], jnp.zeros((), jnp.bfloat16)), axis=2
    )
    send_gate = jnp.sum(
        jnp.where(
            choose, jnp.transpose(gate_tj, (2, 0, 1))[:, :, None, :], jnp.zeros((), jnp.bfloat16)
        ),
        axis=3,
    )
    gate_row = jnp.pad(
        send_gate.reshape(near, 1, planes * capacity),
        ((0, 0), (0, 0), (0, width - planes * capacity)),
    )
    send_x = jnp.einsum(
        "jzrt,ztd->jzrd",
        choose_b,
        seen_x,
        preferred_element_type=jnp.float32,
    ).astype(jnp.bfloat16)
    send_x = jnp.concatenate(
        [send_x.reshape(near, planes * capacity, width), gate_row], axis=1
    )
    send_dy = (
        jnp.einsum("jzrt,ztd->jzrd", choose_b, seen_dy, preferred_element_type=jnp.float32)
        .astype(jnp.bfloat16)
        .reshape(near, planes * capacity, width)
    )
    all_weights = lax.all_gather(
        jnp.concatenate([w_gate, w_up, w_down], axis=2), "dp", axis=1, tiled=True
    )[0]
    gate_proj = all_weights[:, :hidden_units]
    up_proj = all_weights[:, hidden_units : 2 * hidden_units]
    down_proj = all_weights[:, 2 * hidden_units :]
    recv_x = lax.all_to_all(send_x, ("node", "ly"), split_axis=0, concat_axis=0, tiled=True)
    recv_dy = lax.all_to_all(send_dy, ("node", "ly"), split_axis=0, concat_axis=0, tiled=True)
    results = expert_rows(
        recv_x[:, : planes * capacity, :].reshape(slots, width),
        recv_dy.reshape(slots, width),
        recv_x[:, planes * capacity, : planes * capacity].reshape(slots),
        gate_proj,
        up_proj,
        down_proj,
    )
    grad_row = jnp.pad(
        results[1].reshape(near, 1, planes * capacity),
        ((0, 0), (0, 0), (0, half - planes * capacity)),
    )
    back_lo = jnp.concatenate(
        [results[0][:, :half].reshape(near, planes * capacity, half), grad_row], axis=1
    )
    back_hi = results[0][:, half:].reshape(near, planes * capacity, width - half)
    home_lo = lax.all_to_all(back_lo, ("node", "ly"), split_axis=0, concat_axis=0, tiled=True)
    home_gate = home_lo[:, planes * capacity, : planes * capacity].reshape(
        near, planes, capacity
    )
    home_lo = home_lo[:, : planes * capacity, :].reshape(near, planes, capacity, half)
    home_hi = lax.all_to_all(
        back_hi, ("node", "ly"), split_axis=0, concat_axis=0, tiled=True
    ).reshape(near, planes, capacity, width - half)
    partial_lo = jnp.einsum(
        "jzrt,jzrd->ztd", choose_b, home_lo, preferred_element_type=jnp.float32
    )
    gate_jzt = jnp.sum(
        jnp.where(choose, home_gate[..., None], jnp.zeros((), jnp.bfloat16)), axis=2
    )
    pick_gate = jnp.sum(
        jnp.where(
            hit, jnp.transpose(gate_jzt, (1, 2, 0))[:, :, None, :], jnp.zeros((), jnp.bfloat16)
        ),
        axis=3,
    )
    gate_cols = jnp.pad(
        pick_gate.astype(jnp.float32).reshape(planes, 1, tokens_dev * top_count),
        ((0, 0), (0, 0), (0, half - tokens_dev * top_count)),
    )
    summed_down = lax.psum_scatter(results[4], "dp", scatter_dimension=0, tiled=True)
    summed = lax.psum_scatter(
        jnp.concatenate([results[2], results[3]], axis=1), "dp", scatter_dimension=0, tiled=True
    )
    summed_down, summed, partial_lo, gate_cols = lax.optimization_barrier(
        (summed_down, summed, partial_lo, gate_cols)
    )
    reduced_lo = lax.psum_scatter(
        jnp.concatenate([partial_lo, gate_cols], axis=1), "lz", scatter_dimension=0, tiled=True
    )[0]
    partial_hi = jnp.einsum(
        "jzrt,jzrd->ztd", choose_b, home_hi, preferred_element_type=jnp.float32
    )
    reduced_hi = lax.psum_scatter(partial_hi, "lz", scatter_dimension=0, tiled=True)[0]
    input_grad = jnp.concatenate(
        [reduced_lo[:tokens_dev], reduced_hi], axis=1
    ).astype(jnp.bfloat16)
    gate_grad = (
        reduced_lo[tokens_dev, : tokens_dev * top_count]
        .reshape(tokens_dev, top_count)
        .astype(jnp.bfloat16)
    )
    return (
        input_grad,
        gate_grad,
        summed[None, :, :hidden_units],
        summed[None, :, hidden_units : 2 * hidden_units],
        summed_down[None],
    )


def solution(mesh):
    local_size = mesh.shape["local"]
    rows_of = 4 if local_size % 4 == 0 else 1
    split = jax.sharding.Mesh(
        mesh.devices.reshape(
            mesh.shape["dp"], mesh.shape["node"], local_size // rows_of, rows_of
        ),
        ("dp", "node", "lz", "ly"),
    )
    rows = P(("dp", "node", "lz", "ly"), None)
    expert = P(("node", "lz", "ly"), "dp", None)
    return jax.shard_map(
        local,
        mesh=split,
        in_specs=(rows, rows, rows, rows, expert, expert, expert),
        out_specs=(rows, rows, expert, expert, expert),
        check_vma=False,
    )
```
